32 devices in a mesh: pipe: 2 (over core), ep: 16 (over z, y, x).
Axes of the slice: x: 2, y: 2, z: 4, core: 2. Of those that a mesh axis runs over, the one named last changes fastest.
Arguments:
- x_fwd: bfloat16 [2, 1024, 2048], P('pipe', 'ep'), may hold values from -6 to 6
- ids_fwd: int32 [2, 1024, 8], P('pipe', 'ep'), may hold values from 0 to 15, all different within a row; in each aligned block of 64 rows (0 to 63, 64 to 127, ..., all dimensions but the last counted through in order) at most 48 rows name the same one
- route_fwd: float32 [2, 1024, 8], P('pipe', 'ep'), may hold values from 0.05 to 1
- x_bwd: bfloat16 [2, 1024, 2048], P('pipe', 'ep'), may hold values from -6 to 6
- grad_bwd: bfloat16 [2, 1024, 2048], P('pipe', 'ep'), may hold values from -6 to 6
- ids_bwd: int32 [2, 1024, 8], P('pipe', 'ep'), may hold values from 0 to 15, all different within a row; in each aligned block of 64 rows (0 to 63, 64 to 127, ..., all dimensions but the last counted through in order) at most 48 rows name the same one
- route_bwd: float32 [2, 1024, 8], P('pipe', 'ep'), may hold values from 0.05 to 1
- norm_gain: bfloat16 [2, 2048], P('pipe'), may hold values from 0.25 to 1.75
- w_gate: bfloat16 [2, 16, 2048, 768], P('pipe', 'ep'), may hold values from -0.125 to 0.125
- w_up: bfloat16 [2, 16, 2048, 768], P('pipe', 'ep'), may hold values from -0.125 to 0.125
- w_down: bfloat16 [2, 16, 768, 2048], P('pipe', 'ep'), may hold values from -0.21875 to 0.21875
Outputs:
- fwd_next: bfloat16 [2, 1024, 2048], P('pipe', 'ep')
- bwd_prev: bfloat16 [2, 1024, 2048], P('pipe', 'ep')
The draws below stay inside these ranges and needn't reach their ends.
Inputs may be any that keep to these rules, and one draw needn't show every extreme that they name: `ids_fwd`: in each aligned block of 64 tokens of a section, each token names 8 different experts, no expert is named by more than 48 tokens, and in some block one expert is named by exactly 48. `ids_bwd`: as for ids_fwd.
All inputs are finite; a program needn't handle non-finite values.
Results may differ from the reference program's by a relative error of at most 0.0046.
Values may be sent and summed in bfloat16 or wider, within the bound.
No kernel may reach another device: no remote copies, remote signals or barrier semaphores. Data moves between devices by JAX's collectives and lax.ppermute only.
A program may use at most 128 MiB of HBM per device.

```python
import math
import jax
import jax.numpy as jnp
import numpy as np
from jax import lax

D = 2048
FF = 768
TOP = 8
TOK_DEV = 64
SECTIONS = 2
EXPERTS = 16
TOKENS = 1024
CAP = 48
N_EP = 16


def block_scale(stream_key, extent, shards, least, high):
    factor_of = 1.0
    for dim, blocks in shards:
        draws = jax.random.uniform(jax.random.fold_in(jax.random.fold_in(stream_key, 6), dim), (blocks,), jnp.float32, least / len(shards), high / len(shards))
        factor_of = factor_of * jnp.repeat(jnp.exp(draws), extent[dim] // blocks).reshape((-1,) + (1,) * (len(extent) - 1 - dim))
    return factor_of


def shared_out(own_key, own, number, rows, count, top, reach, skew):
    order = jax.random.permutation(own_key, count)
    crowded, usual = shares(count, rows * top, reach, skew, True), shares(count, rows * top, reach, skew, False)
    places = jnp.arange(count)

    def named(tallies, turn):
        used = int((tallies > 0).sum())
        fixed = max(1, used // 4)
        shifted = fixed + (places - fixed + turn * (used - fixed)) % max(1, count - fixed)
        return jnp.zeros((count,), jnp.int32).at[order[jnp.where(places < fixed, places, shifted)]].set(jnp.asarray(tallies, jnp.int32))

    tallies = jnp.where(number % 4 == 0, named(crowded, number // 4), named(usual, number - number // 4 - 1))
    mixed = jax.random.permutation(jax.random.fold_in(own, 3), count)
    donor, receiver = mixed[0:count // 2 * 2:2], mixed[1:count // 2 * 2:2]
    margin = jnp.minimum(tallies[donor] - 1, reach - tallies[receiver]) // 2
    margin = jnp.where((donor == order[0]) | (receiver == order[0]) | (tallies[receiver] == 0), 0, jnp.maximum(margin, 0))
    shifted = jax.random.randint(jax.random.fold_in(own, 4), (count // 2,), 0, 1 << 20) % (margin + 1)
    tallies = tallies.at[donor].add(-shifted).at[receiver].add(shifted)
    members = jnp.searchsorted(jnp.cumsum(tallies), jnp.arange(rows * top), side="right").astype(jnp.int32)
    grid = members.reshape(top, rows).T
    grid = grid[jax.random.permutation(jax.random.fold_in(own, 1), rows)]
    turn = jax.random.randint(jax.random.fold_in(own, 2), (rows, 1), 0, top)
    return jnp.take_along_axis(grid, (jnp.arange(top)[None, :] + turn) % top, axis=1)


def shares(amount, total, reach, skew, full):
    weights = [(1 << 20) // math.isqrt(standing ** skew) + 1 for standing in range(1, amount + 1)]
    largest = reach if full else min(reach, max(-(-total // amount), total * weights[0] // sum(weights)))
    least = 1 if total - largest >= amount - 1 else 0
    given, surplus = [largest] + [least] * (amount - 1), total - largest - least * (amount - 1)
    while surplus > 0:
        movable = [i for i in range(1, amount) if given[i] < largest] or [i for i in range(1, amount) if given[i] < reach]
        whole, budget = sum([weights[i] for i in movable]), surplus
        for i in movable:
            addition = min(reach - given[i], max(1, budget * weights[i] // whole), surplus)
            given[i] = given[i] + addition
            surplus = surplus - addition
    return np.array(given)


def noise(rng, dims, scale, limit, shards=(), kind=jnp.bfloat16):
    values = scale * jax.random.normal(rng, dims, jnp.float32)
    if shards:
        values = values * block_scale(rng, dims, shards, -0.22, 0.18)
    return jnp.clip(values, -limit, limit).astype(kind)


def setup_inputs(seed: int = 0) -> dict:
    arg_keys = jax.random.split(jax.random.key(seed), 12)
    x_fwd = noise(arg_keys[0], (SECTIONS, TOKENS, D), 1.0, 6.0, ((0, 2), (1, 16)))
    ids_fwd_keys = jax.random.split(jax.random.fold_in(arg_keys[1], 1), SECTIONS * TOKENS // TOK_DEV)
    ids_fwd_turns = jax.random.permutation(jax.random.fold_in(arg_keys[1], 3), SECTIONS * TOKENS // TOK_DEV)
    ids_fwd = jax.vmap(lambda own, number: shared_out(jax.random.fold_in(arg_keys[1], 2), own, number, TOK_DEV, EXPERTS, TOP, CAP, 2))(ids_fwd_keys, ids_fwd_turns).reshape((SECTIONS, TOKENS, TOP))
    route_fwd = jnp.clip(jnp.exp(math.log(1.0) - 2.9957323 * jax.random.uniform(arg_keys[2], (SECTIONS, TOKENS, TOP), jnp.float32) ** block_scale(arg_keys[2], (SECTIONS, TOKENS, TOP), ((0, 2), (1, 16)), -0.2, 0.2)), 0.05, 1.0)
    x_bwd = noise(arg_keys[3], (SECTIONS, TOKENS, D), 1.0, 6.0, ((0, 2), (1, 16)))
    grad_bwd = noise(arg_keys[4], (SECTIONS, TOKENS, D), 1.0, 6.0, ((0, 2), (1, 16)))
    ids_bwd_keys = jax.random.split(jax.random.fold_in(arg_keys[5], 1), SECTIONS * TOKENS // TOK_DEV)
    ids_bwd_turns = jax.random.permutation(jax.random.fold_in(arg_keys[5], 3), SECTIONS * TOKENS // TOK_DEV)
    ids_bwd = jax.vmap(lambda own, number: shared_out(jax.random.fold_in(arg_keys[5], 2), own, number, TOK_DEV, EXPERTS, TOP, CAP, 2))(ids_bwd_keys, ids_bwd_turns).reshape((SECTIONS, TOKENS, TOP))
    route_bwd = jnp.clip(jnp.exp(math.log(1.0) - 2.9957323 * jax.random.uniform(arg_keys[6], (SECTIONS, TOKENS, TOP), jnp.float32) ** block_scale(arg_keys[6], (SECTIONS, TOKENS, TOP), ((0, 2), (1, 16)), -0.2, 0.2)), 0.05, 1.0)
    norm_gain = jnp.clip(1.0 + 0.15 * jax.random.normal(arg_keys[7], (SECTIONS, D), jnp.float32), 0.25, 1.75).astype(jnp.bfloat16)
    w_gate = noise(arg_keys[8], (SECTIONS, EXPERTS, D, FF), D ** -0.5, 0.125, ((0, 2), (1, 16)))
    w_up = noise(arg_keys[9], (SECTIONS, EXPERTS, D, FF), D ** -0.5, 0.125, ((0, 2), (1, 16)))
    w_down = noise(arg_keys[10], (SECTIONS, EXPERTS, FF, D), FF ** -0.5, 0.21875, ((0, 2), (1, 16)))
    return dict(x_fwd=x_fwd, ids_fwd=ids_fwd, route_fwd=route_fwd, x_bwd=x_bwd, grad_bwd=grad_bwd, ids_bwd=ids_bwd, route_bwd=route_bwd, norm_gain=norm_gain, w_gate=w_gate, w_up=w_up, w_down=w_down)


EPS = 1e-06

def slot_places(ids, n_exp, cap):
    flat = ids.reshape(-1).astype(jnp.int32)
    onehot = (flat[:, None] == jnp.arange(n_exp, dtype=jnp.int32)[None, :]).astype(jnp.int32)
    before = (jnp.cumsum(onehot, axis=0) - onehot).astype(jnp.int32)
    slot = lax.optimization_barrier(jnp.sum(before * onehot, axis=1)).astype(jnp.int32)
    return (flat * cap + slot).astype(jnp.int32)

def rms_stats(x):
    xf = x.astype(jnp.float32)
    scale = lax.rsqrt(lax.optimization_barrier(jnp.mean(xf * xf, axis=-1, keepdims=True)) + EPS)
    return (xf, scale)

def expert_forward(rows, w_g, w_u, w_d):
    gate = jnp.dot(rows, w_g, preferred_element_type=jnp.float32)
    upper = jnp.dot(rows, w_u, preferred_element_type=jnp.float32)
    act = (jax.nn.silu(gate) * upper).astype(jnp.bfloat16)
    return jnp.dot(act, w_d, preferred_element_type=jnp.float32).astype(jnp.bfloat16)

def expert_backward(rows, cot, w_g, w_u, w_d):
    gate = jnp.dot(rows, w_g, preferred_element_type=jnp.float32)
    upper = jnp.dot(rows, w_u, preferred_element_type=jnp.float32)
    sigma = jax.nn.sigmoid(gate)
    dact = jnp.dot(cot, w_d.T, preferred_element_type=jnp.float32)
    dgate = (dact * upper * sigma * (1.0 + gate * (1.0 - sigma))).astype(jnp.bfloat16)
    dup = (dact * gate * sigma).astype(jnp.bfloat16)
    total = jnp.dot(dgate, w_g.T, preferred_element_type=jnp.float32) + jnp.dot(dup, w_u.T, preferred_element_type=jnp.float32)
    return total.astype(jnp.bfloat16)

def norm_backward(xf, scale, gain, upstream):
    scaled = gain * upstream
    inner = lax.optimization_barrier(jnp.mean(xf * scaled, axis=-1, keepdims=True))
    return scale * scaled - xf * (scale * scale * scale) * inner

def block_places(block):
    return slot_places(block, EXPERTS, CAP)

def tables(ids, route):
    weights = route / lax.optimization_barrier(jnp.sum(route, axis=-1, keepdims=True))
    blocks = ids.reshape(N_EP, TOK_DEV, TOP).astype(jnp.int32)
    places = jax.vmap(block_places)(blocks)
    flat_e = blocks.reshape(N_EP, TOK_DEV * TOP)
    slot = (places - flat_e * CAP).astype(jnp.int32)
    source = jnp.arange(N_EP, dtype=jnp.int32)[:, None]
    column = (source * CAP + slot).astype(jnp.int32)
    token = (source * TOK_DEV + jnp.arange(TOK_DEV * TOP, dtype=jnp.int32)[None, :] // TOP).astype(jnp.int32)
    table = jnp.full((EXPERTS, N_EP * CAP), -1, jnp.int32).at[flat_e, column].set(token)
    wtable = jnp.zeros((EXPERTS, N_EP * CAP), jnp.float32).at[flat_e, column].set(weights.reshape(N_EP, TOK_DEV * TOP))
    return (table, wtable)

def section(operands):
    x_f, ids_f, route_f, x_b, grad_b, ids_b, route_b, gain, w_g, w_u, w_d = operands
    gainf = gain.astype(jnp.float32)
    xf, scale_f = rms_stats(x_f)
    h_f = (xf * scale_f * gainf).astype(jnp.bfloat16)
    xb, scale_b = rms_stats(x_b)
    h_b = (xb * scale_b * gainf).astype(jnp.bfloat16)
    table_f, wtable_f = tables(ids_f, route_f)
    table_b, wtable_b = tables(ids_b, route_b)
    zero_b = jnp.zeros((), jnp.bfloat16)

    def per_expert(carry, expert):
        out_f, out_b = carry
        index = table_f[expert]
        valid = (index >= 0)[:, None]
        safe = jnp.maximum(index, 0)
        rows = jnp.where(valid, h_f[safe], zero_b)
        outcome = expert_forward(rows, w_g[expert], w_u[expert], w_d[expert])
        out_f = out_f.at[safe].add(jnp.where(valid, wtable_f[expert][:, None] * outcome.astype(jnp.float32), 0.0))
        index = table_b[expert]
        valid = (index >= 0)[:, None]
        safe = jnp.maximum(index, 0)
        rows = jnp.where(valid, h_b[safe], zero_b)
        cot = jnp.where(valid, (wtable_b[expert][:, None] * grad_b[safe].astype(jnp.float32)).astype(jnp.bfloat16), zero_b)
        back = expert_backward(rows, cot, w_g[expert], w_u[expert], w_d[expert])
        out_b = out_b.at[safe].add(jnp.where(valid, back.astype(jnp.float32), 0.0))
        return ((out_f, out_b), None)
    start = (jnp.zeros((TOKENS, D), jnp.float32), jnp.zeros((TOKENS, D), jnp.float32))
    (mixed, dnorm), _ = lax.scan(per_expert, start, jnp.arange(EXPERTS, dtype=jnp.int32))
    y = (xf + mixed).astype(jnp.bfloat16)
    dx = (grad_b.astype(jnp.float32) + norm_backward(xb, scale_b, gainf, dnorm)).astype(jnp.bfloat16)
    return (y, dx)

def reference(x_fwd, ids_fwd, route_fwd, x_bwd, grad_bwd, ids_bwd, route_bwd, norm_gain, w_gate, w_up, w_down):
    y, dx = lax.map(section, (x_fwd, ids_fwd, route_fwd, x_bwd, grad_bwd, ids_bwd, route_bwd, norm_gain, w_gate, w_up, w_down))
    return (jnp.roll(y, 1, axis=0), jnp.roll(dx, -1, axis=0))
```

```python
import jax
import jax.numpy as jnp
from jax import lax
from jax.sharding import PartitionSpec as P

EPS = 1e-06


def from_behind(block, axis, distance):
    devices = range(lax.axis_size(axis))
    route = [((i - distance) % len(devices), i) for i in devices]
    return lax.ppermute(block, axis, route)


def slot_places(ids, n_exp, cap):
    flat = ids.reshape(-1)
    onehot = (flat[:, None] == jnp.arange(n_exp, dtype=jnp.int32)[None, :]).astype(jnp.int32)
    before = jnp.cumsum(onehot, axis=0) - onehot
    slot = jnp.sum(before * onehot, axis=1)
    return flat * cap + slot


def rms_stats(x):
    xf = x.astype(jnp.float32)
    scale = lax.rsqrt(jnp.mean(xf * xf, axis=-1, keepdims=True) + EPS)
    return (xf, scale)


def expert_forward(rows, w_g, w_u, w_d):
    gate = jnp.dot(rows, w_g, preferred_element_type=jnp.float32)
    upper = jnp.dot(rows, w_u, preferred_element_type=jnp.float32)
    act = (jax.nn.silu(gate) * upper).astype(jnp.bfloat16)
    return jnp.dot(act, w_d, preferred_element_type=jnp.float32).astype(jnp.bfloat16)


def expert_backward(rows, cot, w_g, w_u, w_d):
    gate = jnp.dot(rows, w_g, preferred_element_type=jnp.float32)
    upper = jnp.dot(rows, w_u, preferred_element_type=jnp.float32)
    sigma = jax.nn.sigmoid(gate)
    dact = jnp.dot(cot, w_d.T, preferred_element_type=jnp.float32)
    dgate = (dact * upper * sigma * (1.0 + gate * (1.0 - sigma))).astype(jnp.bfloat16)
    dup = (dact * gate * sigma).astype(jnp.bfloat16)
    total = jnp.dot(dgate, w_g.T, preferred_element_type=jnp.float32) + jnp.dot(
        dup, w_u.T, preferred_element_type=jnp.float32
    )
    return total.astype(jnp.bfloat16)


def norm_backward(xf, scale, gain, upstream):
    scaled = gain * upstream
    inner = jnp.mean(xf * scaled, axis=-1, keepdims=True)
    return scale * scaled - xf * (scale * scale * scale) * inner


def expert_slots(ids_all, weights_all, me, cap):
    match = ids_all == me
    chosen = jnp.any(match, axis=-1)
    weight = jnp.sum(jnp.where(match, weights_all, 0.0), axis=-1)
    pos = jnp.cumsum(chosen.astype(jnp.int32), axis=1) - chosen.astype(jnp.int32)
    slot = jnp.arange(cap, dtype=jnp.int32)[None, :, None]
    onehot = chosen[:, None, :] & (pos[:, None, :] == slot)
    slot_w = jnp.sum(jnp.where(onehot, weight[:, None, :], 0.0), axis=-1)
    return onehot.astype(jnp.bfloat16), slot_w


def pick_rows(onehot, rows):
    picked = jnp.einsum("bct,btd->bcd", onehot, rows, preferred_element_type=jnp.float32)
    return picked.astype(jnp.bfloat16)


def combine_rows(places, back, top):
    count = back.shape[0]
    onehot = (places[:, None] == jnp.arange(count, dtype=jnp.int32)[None, :]).astype(jnp.bfloat16)
    picked = jnp.dot(onehot, back, preferred_element_type=jnp.float32)
    return picked.reshape(-1, top, back.shape[1])


def local(
    x_fwd, ids_fwd, route_fwd, x_bwd, grad_bwd, ids_bwd, route_bwd, norm_gain, w_gate, w_up, w_down
):
    n_exp = lax.axis_size("ep")
    me = lax.axis_index("ep")
    tok_dev = x_fwd.shape[1]
    width = x_fwd.shape[2]
    top = ids_fwd.shape[2]
    cap = 3 * tok_dev * top // (2 * n_exp)
    gain = norm_gain[0].astype(jnp.float32)
    w_g = w_gate[0, 0]
    w_u = w_up[0, 0]
    w_d = w_down[0, 0]
    xf, scale_f = rms_stats(x_fwd[0])
    h_f = (xf * scale_f * gain).astype(jnp.bfloat16)
    xb, scale_b = rms_stats(x_bwd[0])
    h_b = (xb * scale_b * gain).astype(jnp.bfloat16)
    grad = grad_bwd[0]
    weights_f = route_fwd[0] / jnp.sum(route_fwd[0], axis=-1, keepdims=True)
    weights_b = route_bwd[0] / jnp.sum(route_bwd[0], axis=-1, keepdims=True)

    def gather(v):
        return lax.all_gather(v, "ep", axis=0, tiled=False)

    all_h_f = gather(h_f)
    all_ids_f = gather(ids_fwd[0])
    all_w_f = gather(weights_f)
    all_h_b = gather(h_b)
    all_g = gather(grad)
    all_ids_b = gather(ids_bwd[0])
    all_w_b = gather(weights_b)

    onehot_f, _ = expert_slots(all_ids_f, all_w_f, me, cap)
    rows = pick_rows(onehot_f, all_h_f).reshape(-1, width)
    made_f = expert_forward(rows, w_g, w_u, w_d).reshape(n_exp, cap, width)
    back_f = lax.all_to_all(made_f, "ep", split_axis=0, concat_axis=0, tiled=True)

    onehot_b, slot_w_b = expert_slots(all_ids_b, all_w_b, me, cap)
    rows = pick_rows(onehot_b, all_h_b).reshape(-1, width)
    g_rows = pick_rows(onehot_b, all_g)
    cots = (slot_w_b[:, :, None] * g_rows.astype(jnp.float32)).astype(jnp.bfloat16).reshape(-1, width)
    made_b = expert_backward(rows, cots, w_g, w_u, w_d).reshape(n_exp, cap, width)
    back_b = lax.all_to_all(made_b, "ep", split_axis=0, concat_axis=0, tiled=True)

    places_f = slot_places(ids_fwd[0], n_exp, cap)
    picked_f = combine_rows(places_f, back_f.reshape(-1, width), top)
    mixed = jnp.sum(weights_f[:, :, None] * picked_f, axis=1)
    layer_out = (xf + mixed).astype(jnp.bfloat16)[None]
    places_b = slot_places(ids_bwd[0], n_exp, cap)
    picked_b = combine_rows(places_b, back_b.reshape(-1, width), top)
    dnorm = jnp.sum(picked_b, axis=1)
    input_grad = (grad.astype(jnp.float32) + norm_backward(xb, scale_b, gain, dnorm)).astype(
        jnp.bfloat16
    )[None]
    fwd_next = from_behind(layer_out, "pipe", 1)
    bwd_prev = from_behind(input_grad, "pipe", -1)
    return (fwd_next, bwd_prev)


def solution(mesh):
    placed = (
        P("pipe", "ep", None),
        P("pipe", "ep", None),
        P("pipe", "ep", None),
        P("pipe", "ep", None),
        P("pipe", "ep", None),
        P("pipe", "ep", None),
        P("pipe", "ep", None),
        P("pipe", None),
        P("pipe", "ep", None, None),
        P("pipe", "ep", None, None),
        P("pipe", "ep", None, None),
    )
    return jax.shard_map(
        local,
        mesh=mesh,
        in_specs=placed,
        out_specs=(P("pipe", "ep", None), P("pipe", "ep", None)),
        check_vma=False,
    )
```

```python
import jax
import jax.numpy as jnp
from jax import lax
from jax.sharding import PartitionSpec as P

EPS = 1e-06


def from_behind(block, axis, distance):
    devices = range(lax.axis_size(axis))
    route = [((i - distance) % len(devices), i) for i in devices]
    return lax.ppermute(block, axis, route)


def slot_places(ids, n_exp, cap):
    flat = ids.reshape(-1)
    onehot = (flat[:, None] == jnp.arange(n_exp, dtype=jnp.int32)[None, :]).astype(jnp.int32)
    before = jnp.cumsum(onehot, axis=0) - onehot
    slot = jnp.sum(before * onehot, axis=1)
    return flat * cap + slot


def rms_stats(x):
    xf = x.astype(jnp.float32)
    scale = lax.rsqrt(jnp.mean(xf * xf, axis=-1, keepdims=True) + EPS)
    return (xf, scale)


def expert_forward(rows, w_g, w_u, w_d):
    gate = jnp.dot(rows, w_g, preferred_element_type=jnp.float32)
    upper = jnp.dot(rows, w_u, preferred_element_type=jnp.float32)
    act = (jax.nn.silu(gate) * upper).astype(jnp.bfloat16)
    return jnp.dot(act, w_d, preferred_element_type=jnp.float32).astype(jnp.bfloat16)


def expert_backward(rows, cot, w_g, w_u, w_d):
    gate = jnp.dot(rows, w_g, preferred_element_type=jnp.float32)
    upper = jnp.dot(rows, w_u, preferred_element_type=jnp.float32)
    sigma = jax.nn.sigmoid(gate)
    dact = jnp.dot(cot, w_d.T, preferred_element_type=jnp.float32)
    dgate = (dact * upper * sigma * (1.0 + gate * (1.0 - sigma))).astype(jnp.bfloat16)
    dup = (dact * gate * sigma).astype(jnp.bfloat16)
    total = jnp.dot(dgate, w_g.T, preferred_element_type=jnp.float32) + jnp.dot(
        dup, w_u.T, preferred_element_type=jnp.float32
    )
    return total.astype(jnp.bfloat16)


def norm_backward(xf, scale, gain, upstream):
    scaled = gain * upstream
    inner = jnp.mean(xf * scaled, axis=-1, keepdims=True)
    return scale * scaled - xf * (scale * scale * scale) * inner


def expert_slots(ids_all, weights_all, me, cap):
    match = ids_all == me
    chosen = jnp.any(match, axis=-1)
    weight = jnp.sum(jnp.where(match, weights_all, 0.0), axis=-1)
    pos = jnp.cumsum(chosen.astype(jnp.int32), axis=1) - chosen.astype(jnp.int32)
    slot = jnp.arange(cap, dtype=jnp.int32)[None, :, None]
    onehot = chosen[:, None, :] & (pos[:, None, :] == slot)
    slot_w = jnp.sum(jnp.where(onehot, weight[:, None, :], 0.0), axis=-1)
    return onehot.astype(jnp.bfloat16), slot_w


def pick_rows(onehot, rows):
    picked = jnp.einsum("bct,btd->bcd", onehot, rows, preferred_element_type=jnp.float32)
    return picked.astype(jnp.bfloat16)


def combine_rows(places, back, top):
    count = back.shape[0]
    onehot = (places[:, None] == jnp.arange(count, dtype=jnp.int32)[None, :]).astype(jnp.bfloat16)
    picked = jnp.dot(onehot, back, preferred_element_type=jnp.float32)
    return picked.reshape(-1, top, back.shape[1])


def local(
    x_fwd, ids_fwd, route_fwd, x_bwd, grad_bwd, ids_bwd, route_bwd, norm_gain, w_gate, w_up, w_down
):
    n_exp = lax.axis_size("ep")
    me = lax.axis_index("ep")
    tok_dev = x_fwd.shape[1]
    width = x_fwd.shape[2]
    top = ids_fwd.shape[2]
    cap = 3 * tok_dev * top // (2 * n_exp)
    gain = norm_gain[0].astype(jnp.float32)
    w_g = w_gate[0, 0]
    w_u = w_up[0, 0]
    w_d = w_down[0, 0]
    xf, scale_f = rms_stats(x_fwd[0])
    h_f = (xf * scale_f * gain).astype(jnp.bfloat16)
    xb, scale_b = rms_stats(x_bwd[0])
    h_b = (xb * scale_b * gain).astype(jnp.bfloat16)
    grad = grad_bwd[0]
    weights_f = route_fwd[0] / jnp.sum(route_fwd[0], axis=-1, keepdims=True)
    weights_b = route_bwd[0] / jnp.sum(route_bwd[0], axis=-1, keepdims=True)

    def gather(v):
        return lax.all_gather(v, "ep", axis=0, tiled=False)

    tables = gather(
        jnp.concatenate(
            [ids_fwd[0].astype(jnp.float32), route_fwd[0], ids_bwd[0].astype(jnp.float32), route_bwd[0]],
            axis=-1,
        )
    )
    all_ids_f = tables[..., 0:top].astype(jnp.int32)
    all_route_f = tables[..., top:2 * top]
    all_ids_b = tables[..., 2 * top:3 * top].astype(jnp.int32)
    all_route_b = tables[..., 3 * top:4 * top]
    all_w_f = all_route_f / jnp.sum(all_route_f, axis=-1, keepdims=True)
    all_w_b = all_route_b / jnp.sum(all_route_b, axis=-1, keepdims=True)
    all_h_f = gather(h_f)
    all_h_b = gather(h_b)
    all_g = gather(grad)

    onehot_f, _ = expert_slots(all_ids_f, all_w_f, me, cap)
    rows = pick_rows(onehot_f, all_h_f).reshape(-1, width)
    made_f = expert_forward(rows, w_g, w_u, w_d).reshape(n_exp, cap, width)
    back_f = lax.all_to_all(made_f, "ep", split_axis=0, concat_axis=0, tiled=True)

    onehot_b, slot_w_b = expert_slots(all_ids_b, all_w_b, me, cap)
    rows = pick_rows(onehot_b, all_h_b).reshape(-1, width)
    g_rows = pick_rows(onehot_b, all_g)
    cots = (slot_w_b[:, :, None] * g_rows.astype(jnp.float32)).astype(jnp.bfloat16).reshape(-1, width)
    made_b = expert_backward(rows, cots, w_g, w_u, w_d).reshape(n_exp, cap, width)
    back_b = lax.all_to_all(made_b, "ep", split_axis=0, concat_axis=0, tiled=True)

    places_f = slot_places(ids_fwd[0], n_exp, cap)
    picked_f = combine_rows(places_f, back_f.reshape(-1, width), top)
    mixed = jnp.sum(weights_f[:, :, None] * picked_f, axis=1)
    layer_out = (xf + mixed).astype(jnp.bfloat16)[None]
    places_b = slot_places(ids_bwd[0], n_exp, cap)
    picked_b = combine_rows(places_b, back_b.reshape(-1, width), top)
    dnorm = jnp.sum(picked_b, axis=1)
    input_grad = (grad.astype(jnp.float32) + norm_backward(xb, scale_b, gain, dnorm)).astype(
        jnp.bfloat16
    )[None]
    fwd_next = from_behind(layer_out, "pipe", 1)
    bwd_prev = from_behind(input_grad, "pipe", -1)
    return (fwd_next, bwd_prev)


def solution(mesh):
    placed = (
        P("pipe", "ep", None),
        P("pipe", "ep", None),
        P("pipe", "ep", None),
        P("pipe", "ep", None),
        P("pipe", "ep", None),
        P("pipe", "ep", None),
        P("pipe", "ep", None),
        P("pipe", None),
        P("pipe", "ep", None, None),
        P("pipe", "ep", None, None),
        P("pipe", "ep", None, None),
    )
    return jax.shard_map(
        local,
        mesh=mesh,
        in_specs=placed,
        out_specs=(P("pipe", "ep", None), P("pipe", "ep", None)),
        check_vma=False,
    )
```

```python
import jax
import jax.numpy as jnp
from jax import lax
from jax.sharding import PartitionSpec as P

EPS = 1e-06


def from_behind(block, axis, distance):
    devices = range(lax.axis_size(axis))
    route = [((i - distance) % len(devices), i) for i in devices]
    return lax.ppermute(block, axis, route)


def slot_places(ids, n_exp, cap):
    flat = ids.reshape(-1)
    onehot = (flat[:, None] == jnp.arange(n_exp, dtype=jnp.int32)[None, :]).astype(jnp.int32)
    before = jnp.cumsum(onehot, axis=0) - onehot
    slot = jnp.sum(before * onehot, axis=1)
    return flat * cap + slot


def rms_stats(x):
    xf = x.astype(jnp.float32)
    scale = lax.rsqrt(jnp.mean(xf * xf, axis=-1, keepdims=True) + EPS)
    return (xf, scale)


def expert_forward(rows, w_g, w_u, w_d):
    gate = jnp.dot(rows, w_g, preferred_element_type=jnp.float32)
    upper = jnp.dot(rows, w_u, preferred_element_type=jnp.float32)
    act = (jax.nn.silu(gate) * upper).astype(jnp.bfloat16)
    return jnp.dot(act, w_d, preferred_element_type=jnp.float32).astype(jnp.bfloat16)


def expert_backward(rows, cot, w_g, w_u, w_d):
    gate = jnp.dot(rows, w_g, preferred_element_type=jnp.float32)
    upper = jnp.dot(rows, w_u, preferred_element_type=jnp.float32)
    sigma = jax.nn.sigmoid(gate)
    dact = jnp.dot(cot, w_d.T, preferred_element_type=jnp.float32)
    dgate = (dact * upper * sigma * (1.0 + gate * (1.0 - sigma))).astype(jnp.bfloat16)
    dup = (dact * gate * sigma).astype(jnp.bfloat16)
    total = jnp.dot(dgate, w_g.T, preferred_element_type=jnp.float32) + jnp.dot(
        dup, w_u.T, preferred_element_type=jnp.float32
    )
    return total.astype(jnp.bfloat16)


def norm_backward(xf, scale, gain, upstream):
    scaled = gain * upstream
    inner = jnp.mean(xf * scaled, axis=-1, keepdims=True)
    return scale * scaled - xf * (scale * scale * scale) * inner


def expert_slots(ids_all, weights_all, me, cap):
    match = ids_all == me
    chosen = jnp.any(match, axis=-1)
    weight = jnp.sum(jnp.where(match, weights_all, 0.0), axis=-1)
    pos = jnp.cumsum(chosen.astype(jnp.int32), axis=1) - chosen.astype(jnp.int32)
    slot = jnp.arange(cap, dtype=jnp.int32)[None, :, None]
    onehot = chosen[:, None, :] & (pos[:, None, :] == slot)
    slot_w = jnp.sum(jnp.where(onehot, weight[:, None, :], 0.0), axis=-1)
    return onehot.astype(jnp.bfloat16), slot_w


def pick_rows(onehot, rows):
    picked = jnp.einsum("bct,btd->bcd", onehot, rows, preferred_element_type=jnp.float32)
    return picked.astype(jnp.bfloat16)


def combine_rows(places, back, top):
    count = back.shape[0]
    onehot = (places[:, None] == jnp.arange(count, dtype=jnp.int32)[None, :]).astype(jnp.bfloat16)
    picked = jnp.dot(onehot, back, preferred_element_type=jnp.float32)
    return picked.reshape(-1, top, back.shape[1])


def _pairs(n, n2, stage, move):
    out = []
    for i in range(n):
        e1, e2 = i // n2, i % n2
        if stage == 1:
            e1 = move(e1)
        else:
            e2 = move(e2)
        out.append((i, e1 * n2 + e2))
    return out


def gather_ep(v, axis_name):
    n = lax.axis_size(axis_name)
    n2 = 4
    if n % n2 or v.shape[0] % 2:
        return lax.all_gather(v, axis_name, axis=0, tiled=False)
    n1 = n // n2
    me = lax.axis_index(axis_name)
    e1, e2 = me // n2, me % n2
    s1 = jnp.zeros((n1,) + v.shape, v.dtype)
    s1 = lax.dynamic_update_index_in_dim(s1, v, e1, 0)
    for d in range(1, n1):
        got = lax.ppermute(v, axis_name, _pairs(n, n2, 1, lambda a: (a + d) % n1))
        s1 = lax.dynamic_update_index_in_dim(s1, got, (e1 - d) % n1, 0)
    flip_x = lambda a: a ^ 1
    flip_y = lambda a: a ^ 2
    px = lax.ppermute(s1, axis_name, _pairs(n, n2, 2, flip_x))
    py = lax.ppermute(s1, axis_name, _pairs(n, n2, 2, flip_y))
    h = v.shape[0] // 2
    d1 = lax.ppermute(px[:, :h], axis_name, _pairs(n, n2, 2, flip_y))
    d2 = lax.ppermute(py[:, h:], axis_name, _pairs(n, n2, 2, flip_x))
    diag = jnp.concatenate([d1, d2], axis=1)
    s2 = jnp.zeros((n2,) + s1.shape, v.dtype)
    s2 = lax.dynamic_update_index_in_dim(s2, s1, e2, 0)
    s2 = lax.dynamic_update_index_in_dim(s2, px, e2 ^ 1, 0)
    s2 = lax.dynamic_update_index_in_dim(s2, py, e2 ^ 2, 0)
    s2 = lax.dynamic_update_index_in_dim(s2, diag, e2 ^ 3, 0)
    return jnp.swapaxes(s2, 0, 1).reshape((n,) + v.shape)


def local(
    x_fwd, ids_fwd, route_fwd, x_bwd, grad_bwd, ids_bwd, route_bwd, norm_gain, w_gate, w_up, w_down
):
    n_exp = lax.axis_size("ep")
    me = lax.axis_index("ep")
    tok_dev = x_fwd.shape[1]
    width = x_fwd.shape[2]
    top = ids_fwd.shape[2]
    cap = 3 * tok_dev * top // (2 * n_exp)
    gain = norm_gain[0].astype(jnp.float32)
    w_g = w_gate[0, 0]
    w_u = w_up[0, 0]
    w_d = w_down[0, 0]
    xf, scale_f = rms_stats(x_fwd[0])
    h_f = (xf * scale_f * gain).astype(jnp.bfloat16)
    xb, scale_b = rms_stats(x_bwd[0])
    h_b = (xb * scale_b * gain).astype(jnp.bfloat16)
    grad = grad_bwd[0]
    weights_f = route_fwd[0] / jnp.sum(route_fwd[0], axis=-1, keepdims=True)
    weights_b = route_bwd[0] / jnp.sum(route_bwd[0], axis=-1, keepdims=True)

    def gather(v):
        return gather_ep(v, "ep")

    tables = gather(
        jnp.concatenate(
            [ids_fwd[0].astype(jnp.float32), route_fwd[0], ids_bwd[0].astype(jnp.float32), route_bwd[0]],
            axis=-1,
        )
    )
    all_ids_f = tables[..., 0:top].astype(jnp.int32)
    all_route_f = tables[..., top:2 * top]
    all_ids_b = tables[..., 2 * top:3 * top].astype(jnp.int32)
    all_route_b = tables[..., 3 * top:4 * top]
    all_w_f = all_route_f / jnp.sum(all_route_f, axis=-1, keepdims=True)
    all_w_b = all_route_b / jnp.sum(all_route_b, axis=-1, keepdims=True)
    all_h_f = gather(h_f)
    both_b = gather(jnp.concatenate([h_b, grad], axis=-1))
    all_h_b = both_b[..., :width]
    all_g = both_b[..., width:]

    onehot_f, _ = expert_slots(all_ids_f, all_w_f, me, cap)
    rows = pick_rows(onehot_f, all_h_f).reshape(-1, width)
    made_f = expert_forward(rows, w_g, w_u, w_d).reshape(n_exp, cap, width)
    back_f = lax.all_to_all(made_f, "ep", split_axis=0, concat_axis=0, tiled=True)

    onehot_b, slot_w_b = expert_slots(all_ids_b, all_w_b, me, cap)
    rows = pick_rows(onehot_b, all_h_b).reshape(-1, width)
    g_rows = pick_rows(onehot_b, all_g)
    cots = (slot_w_b[:, :, None] * g_rows.astype(jnp.float32)).astype(jnp.bfloat16).reshape(-1, width)
    made_b = expert_backward(rows, cots, w_g, w_u, w_d).reshape(n_exp, cap, width)
    back_b = lax.all_to_all(made_b, "ep", split_axis=0, concat_axis=0, tiled=True)

    places_f = slot_places(ids_fwd[0], n_exp, cap)
    picked_f = combine_rows(places_f, back_f.reshape(-1, width), top)
    mixed = jnp.sum(weights_f[:, :, None] * picked_f, axis=1)
    layer_out = (xf + mixed).astype(jnp.bfloat16)[None]
    places_b = slot_places(ids_bwd[0], n_exp, cap)
    picked_b = combine_rows(places_b, back_b.reshape(-1, width), top)
    dnorm = jnp.sum(picked_b, axis=1)
    input_grad = (grad.astype(jnp.float32) + norm_backward(xb, scale_b, gain, dnorm)).astype(
        jnp.bfloat16
    )[None]
    fwd_next = from_behind(layer_out, "pipe", 1)
    bwd_prev = from_behind(input_grad, "pipe", -1)
    return (fwd_next, bwd_prev)


def solution(mesh):
    placed = (
        P("pipe", "ep", None),
        P("pipe", "ep", None),
        P("pipe", "ep", None),
        P("pipe", "ep", None),
        P("pipe", "ep", None),
        P("pipe", "ep", None),
        P("pipe", "ep", None),
        P("pipe", None),
        P("pipe", "ep", None, None),
        P("pipe", "ep", None, None),
        P("pipe", "ep", None, None),
    )
    return jax.shard_map(
        local,
        mesh=mesh,
        in_specs=placed,
        out_specs=(P("pipe", "ep", None), P("pipe", "ep", None)),
        check_vma=False,
    )
```

```python
import jax
import jax.numpy as jnp
from jax import lax
from jax.sharding import PartitionSpec as P

EPS = 1e-06


def from_behind(block, axis, distance):
    devices = range(lax.axis_size(axis))
    route = [((i - distance) % len(devices), i) for i in devices]
    return lax.ppermute(block, axis, route)


def slot_places(ids, n_exp, cap):
    flat = ids.reshape(-1)
    onehot = (flat[:, None] == jnp.arange(n_exp, dtype=jnp.int32)[None, :]).astype(jnp.int32)
    before = jnp.cumsum(onehot, axis=0) - onehot
    slot = jnp.sum(before * onehot, axis=1)
    return flat * cap + slot


def rms_stats(x):
    xf = x.astype(jnp.float32)
    scale = lax.rsqrt(jnp.mean(xf * xf, axis=-1, keepdims=True) + EPS)
    return (xf, scale)


def expert_forward(rows, w_g, w_u, w_d):
    gate = jnp.dot(rows, w_g, preferred_element_type=jnp.float32)
    upper = jnp.dot(rows, w_u, preferred_element_type=jnp.float32)
    act = (jax.nn.silu(gate) * upper).astype(jnp.bfloat16)
    return jnp.dot(act, w_d, preferred_element_type=jnp.float32).astype(jnp.bfloat16)


def expert_backward(rows, cot, w_g, w_u, w_d):
    gate = jnp.dot(rows, w_g, preferred_element_type=jnp.float32)
    upper = jnp.dot(rows, w_u, preferred_element_type=jnp.float32)
    sigma = jax.nn.sigmoid(gate)
    dact = jnp.dot(cot, w_d.T, preferred_element_type=jnp.float32)
    dgate = (dact * upper * sigma * (1.0 + gate * (1.0 - sigma))).astype(jnp.bfloat16)
    dup = (dact * gate * sigma).astype(jnp.bfloat16)
    total = jnp.dot(dgate, w_g.T, preferred_element_type=jnp.float32) + jnp.dot(
        dup, w_u.T, preferred_element_type=jnp.float32
    )
    return total.astype(jnp.bfloat16)


def norm_backward(xf, scale, gain, upstream):
    scaled = gain * upstream
    inner = jnp.mean(xf * scaled, axis=-1, keepdims=True)
    return scale * scaled - xf * (scale * scale * scale) * inner


def expert_slots(ids_all, weights_all, me, cap):
    match = ids_all == me
    chosen = jnp.any(match, axis=-1)
    weight = jnp.sum(jnp.where(match, weights_all, 0.0), axis=-1)
    pos = jnp.cumsum(chosen.astype(jnp.int32), axis=1) - chosen.astype(jnp.int32)
    slot = jnp.arange(cap, dtype=jnp.int32)[None, :, None]
    onehot = chosen[:, None, :] & (pos[:, None, :] == slot)
    slot_w = jnp.sum(jnp.where(onehot, weight[:, None, :], 0.0), axis=-1)
    return onehot.astype(jnp.bfloat16), slot_w


def pick_rows(onehot, rows):
    picked = jnp.einsum("bct,btd->bcd", onehot, rows, preferred_element_type=jnp.float32)
    return picked.astype(jnp.bfloat16)


def combine_rows(places, back, top):
    count = back.shape[0]
    onehot = (places[:, None] == jnp.arange(count, dtype=jnp.int32)[None, :]).astype(jnp.bfloat16)
    picked = jnp.dot(onehot, back, preferred_element_type=jnp.float32)
    return picked.reshape(-1, top, back.shape[1])


def _pairs(n, n2, stage, move):
    out = []
    for i in range(n):
        e1, e2 = i // n2, i % n2
        if stage == 1:
            e1 = move(e1)
        else:
            e2 = move(e2)
        out.append((i, e1 * n2 + e2))
    return out


def gather_ep(v, axis_name):
    n = lax.axis_size(axis_name)
    n2 = 4
    if n % n2 or v.shape[0] % 2:
        return lax.all_gather(v, axis_name, axis=0, tiled=False)
    n1 = n // n2
    me = lax.axis_index(axis_name)
    e1, e2 = me // n2, me % n2
    s1 = jnp.zeros((n1,) + v.shape, v.dtype)
    s1 = lax.dynamic_update_index_in_dim(s1, v, e1, 0)
    for d in range(1, n1):
        got = lax.ppermute(v, axis_name, _pairs(n, n2, 1, lambda a: (a + d) % n1))
        s1 = lax.dynamic_update_index_in_dim(s1, got, (e1 - d) % n1, 0)
    flip_x = lambda a: a ^ 1
    flip_y = lambda a: a ^ 2
    px = lax.ppermute(s1, axis_name, _pairs(n, n2, 2, flip_x))
    py = lax.ppermute(s1, axis_name, _pairs(n, n2, 2, flip_y))
    h = v.shape[0] // 2
    d1 = lax.ppermute(px[:, :h], axis_name, _pairs(n, n2, 2, flip_y))
    d2 = lax.ppermute(py[:, h:], axis_name, _pairs(n, n2, 2, flip_x))
    diag = jnp.concatenate([d1, d2], axis=1)
    s2 = jnp.zeros((n2,) + s1.shape, v.dtype)
    s2 = lax.dynamic_update_index_in_dim(s2, s1, e2, 0)
    s2 = lax.dynamic_update_index_in_dim(s2, px, e2 ^ 1, 0)
    s2 = lax.dynamic_update_index_in_dim(s2, py, e2 ^ 2, 0)
    s2 = lax.dynamic_update_index_in_dim(s2, diag, e2 ^ 3, 0)
    return jnp.swapaxes(s2, 0, 1).reshape((n,) + v.shape)


def local(
    x_fwd, ids_fwd, route_fwd, x_bwd, grad_bwd, ids_bwd, route_bwd, norm_gain, w_gate, w_up, w_down
):
    n_exp = lax.axis_size("ep")
    me = lax.axis_index("ep")
    tok_dev = x_fwd.shape[1]
    width = x_fwd.shape[2]
    top = ids_fwd.shape[2]
    cap = 3 * tok_dev * top // (2 * n_exp)
    gain = norm_gain[0].astype(jnp.float32)
    w_g = w_gate[0, 0]
    w_u = w_up[0, 0]
    w_d = w_down[0, 0]
    xf, scale_f = rms_stats(x_fwd[0])
    h_f = (xf * scale_f * gain).astype(jnp.bfloat16)
    xb, scale_b = rms_stats(x_bwd[0])
    h_b = (xb * scale_b * gain).astype(jnp.bfloat16)
    grad = grad_bwd[0]
    weights_f = route_fwd[0] / jnp.sum(route_fwd[0], axis=-1, keepdims=True)
    weights_b = route_bwd[0] / jnp.sum(route_bwd[0], axis=-1, keepdims=True)

    def split3(r):
        hi = lax.reduce_precision(r, exponent_bits=8, mantissa_bits=7)
        rest = r - hi
        mid = lax.reduce_precision(rest, exponent_bits=8, mantissa_bits=7)
        return jnp.concatenate([hi, mid, rest - mid], axis=-1).astype(jnp.bfloat16)

    def join3(p):
        p = p.astype(jnp.float32)
        return (p[..., 0:top] + p[..., top:2 * top]) + p[..., 2 * top:3 * top]

    meta = jnp.concatenate(
        [ids_fwd[0].astype(jnp.bfloat16), ids_bwd[0].astype(jnp.bfloat16), split3(route_fwd[0]), split3(route_bwd[0])],
        axis=-1,
    )
    pad = (-meta.shape[-1]) % 128
    meta = jnp.concatenate([meta, jnp.zeros((tok_dev, pad), jnp.bfloat16)], axis=-1)
    message = gather_ep(jnp.concatenate([h_f, h_b, grad, meta], axis=-1), "ep")
    all_h_f = message[..., 0:width]
    all_h_b = message[..., width:2 * width]
    all_g = message[..., 2 * width:3 * width]
    got = message[..., 3 * width:]
    all_ids_f = got[..., 0:top].astype(jnp.int32)
    all_ids_b = got[..., top:2 * top].astype(jnp.int32)
    all_route_f = join3(got[..., 2 * top:5 * top])
    all_route_b = join3(got[..., 5 * top:8 * top])
    all_w_f = all_route_f / jnp.sum(all_route_f, axis=-1, keepdims=True)
    all_w_b = all_route_b / jnp.sum(all_route_b, axis=-1, keepdims=True)

    onehot_f, _ = expert_slots(all_ids_f, all_w_f, me, cap)
    rows = pick_rows(onehot_f, all_h_f).reshape(-1, width)
    made_f = expert_forward(rows, w_g, w_u, w_d).reshape(n_exp, cap, width)
    back_f = lax.all_to_all(made_f, "ep", split_axis=0, concat_axis=0, tiled=True)

    onehot_b, slot_w_b = expert_slots(all_ids_b, all_w_b, me, cap)
    rows = pick_rows(onehot_b, all_h_b).reshape(-1, width)
    g_rows = pick_rows(onehot_b, all_g)
    cots = (slot_w_b[:, :, None] * g_rows.astype(jnp.float32)).astype(jnp.bfloat16).reshape(-1, width)
    made_b = expert_backward(rows, cots, w_g, w_u, w_d).reshape(n_exp, cap, width)
    back_b = lax.all_to_all(made_b, "ep", split_axis=0, concat_axis=0, tiled=True)

    places_f = slot_places(ids_fwd[0], n_exp, cap)
    picked_f = combine_rows(places_f, back_f.reshape(-1, width), top)
    mixed = jnp.sum(weights_f[:, :, None] * picked_f, axis=1)
    layer_out = (xf + mixed).astype(jnp.bfloat16)[None]
    places_b = slot_places(ids_bwd[0], n_exp, cap)
    picked_b = combine_rows(places_b, back_b.reshape(-1, width), top)
    dnorm = jnp.sum(picked_b, axis=1)
    input_grad = (grad.astype(jnp.float32) + norm_backward(xb, scale_b, gain, dnorm)).astype(
        jnp.bfloat16
    )[None]
    fwd_next = from_behind(layer_out, "pipe", 1)
    bwd_prev = from_behind(input_grad, "pipe", -1)
    return (fwd_next, bwd_prev)


def solution(mesh):
    placed = (
        P("pipe", "ep", None),
        P("pipe", "ep", None),
        P("pipe", "ep", None),
        P("pipe", "ep", None),
        P("pipe", "ep", None),
        P("pipe", "ep", None),
        P("pipe", "ep", None),
        P("pipe", None),
        P("pipe", "ep", None, None),
        P("pipe", "ep", None, None),
        P("pipe", "ep", None, None),
    )
    return jax.shard_map(
        local,
        mesh=mesh,
        in_specs=placed,
        out_specs=(P("pipe", "ep", None), P("pipe", "ep", None)),
        check_vma=False,
    )
```

```python
import jax
import jax.numpy as jnp
from jax import lax
from jax.sharding import PartitionSpec as P

EPS = 1e-06


def from_behind(block, axis, distance):
    devices = range(lax.axis_size(axis))
    route = [((i - distance) % len(devices), i) for i in devices]
    return lax.ppermute(block, axis, route)


def slot_places(ids, n_exp, cap):
    flat = ids.reshape(-1)
    onehot = (flat[:, None] == jnp.arange(n_exp, dtype=jnp.int32)[None, :]).astype(jnp.int32)
    before = jnp.cumsum(onehot, axis=0) - onehot
    slot = jnp.sum(before * onehot, axis=1)
    return flat * cap + slot


def rms_stats(x):
    xf = x.astype(jnp.float32)
    scale = lax.rsqrt(jnp.mean(xf * xf, axis=-1, keepdims=True) + EPS)
    return (xf, scale)


def expert_forward(rows, w_g, w_u, w_d):
    gate = jnp.dot(rows, w_g, preferred_element_type=jnp.float32)
    upper = jnp.dot(rows, w_u, preferred_element_type=jnp.float32)
    act = (jax.nn.silu(gate) * upper).astype(jnp.bfloat16)
    return jnp.dot(act, w_d, preferred_element_type=jnp.float32).astype(jnp.bfloat16)


def expert_backward(rows, cot, w_g, w_u, w_d):
    gate = jnp.dot(rows, w_g, preferred_element_type=jnp.float32)
    upper = jnp.dot(rows, w_u, preferred_element_type=jnp.float32)
    sigma = jax.nn.sigmoid(gate)
    dact = jnp.dot(cot, w_d.T, preferred_element_type=jnp.float32)
    dgate = (dact * upper * sigma * (1.0 + gate * (1.0 - sigma))).astype(jnp.bfloat16)
    dup = (dact * gate * sigma).astype(jnp.bfloat16)
    total = jnp.dot(dgate, w_g.T, preferred_element_type=jnp.float32) + jnp.dot(
        dup, w_u.T, preferred_element_type=jnp.float32
    )
    return total.astype(jnp.bfloat16)


def norm_backward(xf, scale, gain, upstream):
    scaled = gain * upstream
    inner = jnp.mean(xf * scaled, axis=-1, keepdims=True)
    return scale * scaled - xf * (scale * scale * scale) * inner


def expert_slots(ids_all, weights_all, me, cap):
    match = ids_all == me
    chosen = jnp.any(match, axis=-1)
    weight = jnp.sum(jnp.where(match, weights_all, 0.0), axis=-1)
    pos = jnp.cumsum(chosen.astype(jnp.int32), axis=1) - chosen.astype(jnp.int32)
    slot = jnp.arange(cap, dtype=jnp.int32)[None, :, None]
    onehot = chosen[:, None, :] & (pos[:, None, :] == slot)
    slot_w = jnp.sum(jnp.where(onehot, weight[:, None, :], 0.0), axis=-1)
    return onehot.astype(jnp.bfloat16), slot_w


def pick_rows(onehot, rows):
    picked = jnp.einsum("bct,btd->bcd", onehot, rows, preferred_element_type=jnp.float32)
    return picked.astype(jnp.bfloat16)


def combine_rows(places, back, top):
    count = back.shape[0]
    onehot = (places[:, None] == jnp.arange(count, dtype=jnp.int32)[None, :]).astype(jnp.bfloat16)
    picked = jnp.dot(onehot, back, preferred_element_type=jnp.float32)
    return picked.reshape(-1, top, back.shape[1])


def _pairs(n, n2, stage, move):
    out = []
    for i in range(n):
        e1, e2 = i // n2, i % n2
        if stage == 1:
            e1 = move(e1)
        else:
            e2 = move(e2)
        out.append((i, e1 * n2 + e2))
    return out


def gather_ep(v, axis_name):
    n = lax.axis_size(axis_name)
    n2 = 4
    if n % n2 or v.shape[0] % 2:
        return lax.all_gather(v, axis_name, axis=0, tiled=False)
    n1 = n // n2
    me = lax.axis_index(axis_name)
    e1, e2 = me // n2, me % n2
    s1 = jnp.zeros((n1,) + v.shape, v.dtype)
    s1 = lax.dynamic_update_index_in_dim(s1, v, e1, 0)
    for d in range(1, n1):
        got = lax.ppermute(v, axis_name, _pairs(n, n2, 1, lambda a: (a + d) % n1))
        s1 = lax.dynamic_update_index_in_dim(s1, got, (e1 - d) % n1, 0)
    flip_x = lambda a: a ^ 1
    flip_y = lambda a: a ^ 2
    px = lax.ppermute(s1, axis_name, _pairs(n, n2, 2, flip_x))
    py = lax.ppermute(s1, axis_name, _pairs(n, n2, 2, flip_y))
    h = v.shape[0] // 2
    d1 = lax.ppermute(px[:, :h], axis_name, _pairs(n, n2, 2, flip_y))
    d2 = lax.ppermute(py[:, h:], axis_name, _pairs(n, n2, 2, flip_x))
    diag = jnp.concatenate([d1, d2], axis=1)
    s2 = jnp.zeros((n2,) + s1.shape, v.dtype)
    s2 = lax.dynamic_update_index_in_dim(s2, s1, e2, 0)
    s2 = lax.dynamic_update_index_in_dim(s2, px, e2 ^ 1, 0)
    s2 = lax.dynamic_update_index_in_dim(s2, py, e2 ^ 2, 0)
    s2 = lax.dynamic_update_index_in_dim(s2, diag, e2 ^ 3, 0)
    return jnp.swapaxes(s2, 0, 1).reshape((n,) + v.shape)


def exchange_ep(blocks, axis_name):
    n = lax.axis_size(axis_name)
    me = lax.axis_index(axis_name)
    out = lax.dynamic_update_index_in_dim(
        jnp.zeros_like(blocks), lax.dynamic_index_in_dim(blocks, me, 0, keepdims=False), me, 0
    )
    for d in range(1, n):
        part = lax.dynamic_index_in_dim(blocks, (me + d) % n, 0, keepdims=False)
        got = lax.ppermute(part, axis_name, [(i, (i + d) % n) for i in range(n)])
        out = lax.dynamic_update_index_in_dim(out, got, (me - d) % n, 0)
    return out


def local(
    x_fwd, ids_fwd, route_fwd, x_bwd, grad_bwd, ids_bwd, route_bwd, norm_gain, w_gate, w_up, w_down
):
    n_exp = lax.axis_size("ep")
    me = lax.axis_index("ep")
    tok_dev = x_fwd.shape[1]
    width = x_fwd.shape[2]
    top = ids_fwd.shape[2]
    cap = 3 * tok_dev * top // (2 * n_exp)
    gain = norm_gain[0].astype(jnp.float32)
    w_g = w_gate[0, 0]
    w_u = w_up[0, 0]
    w_d = w_down[0, 0]
    xf, scale_f = rms_stats(x_fwd[0])
    h_f = (xf * scale_f * gain).astype(jnp.bfloat16)
    xb, scale_b = rms_stats(x_bwd[0])
    h_b = (xb * scale_b * gain).astype(jnp.bfloat16)
    grad = grad_bwd[0]
    weights_f = route_fwd[0] / jnp.sum(route_fwd[0], axis=-1, keepdims=True)
    weights_b = route_bwd[0] / jnp.sum(route_bwd[0], axis=-1, keepdims=True)

    def split3(r):
        hi = lax.reduce_precision(r, exponent_bits=8, mantissa_bits=7)
        rest = r - hi
        mid = lax.reduce_precision(rest, exponent_bits=8, mantissa_bits=7)
        return jnp.concatenate([hi, mid, rest - mid], axis=-1).astype(jnp.bfloat16)

    def join3(p):
        p = p.astype(jnp.float32)
        return (p[..., 0:top] + p[..., top:2 * top]) + p[..., 2 * top:3 * top]

    meta = jnp.concatenate(
        [ids_fwd[0].astype(jnp.bfloat16), ids_bwd[0].astype(jnp.bfloat16), split3(route_fwd[0]), split3(route_bwd[0])],
        axis=-1,
    )
    pad = (-meta.shape[-1]) % 128
    meta = jnp.concatenate([meta, jnp.zeros((tok_dev, pad), jnp.bfloat16)], axis=-1)
    message = gather_ep(jnp.concatenate([h_f, h_b, grad, meta], axis=-1), "ep")
    all_h_f = message[..., 0:width]
    all_h_b = message[..., width:2 * width]
    all_g = message[..., 2 * width:3 * width]
    got = message[..., 3 * width:]
    all_ids_f = got[..., 0:top].astype(jnp.int32)
    all_ids_b = got[..., top:2 * top].astype(jnp.int32)
    all_route_f = join3(got[..., 2 * top:5 * top])
    all_route_b = join3(got[..., 5 * top:8 * top])
    all_w_f = all_route_f / jnp.sum(all_route_f, axis=-1, keepdims=True)
    all_w_b = all_route_b / jnp.sum(all_route_b, axis=-1, keepdims=True)

    onehot_f, _ = expert_slots(all_ids_f, all_w_f, me, cap)
    rows = pick_rows(onehot_f, all_h_f).reshape(-1, width)
    made_f = expert_forward(rows, w_g, w_u, w_d).reshape(n_exp, cap, width)
    back_f = exchange_ep(made_f, "ep")

    onehot_b, slot_w_b = expert_slots(all_ids_b, all_w_b, me, cap)
    rows = pick_rows(onehot_b, all_h_b).reshape(-1, width)
    g_rows = pick_rows(onehot_b, all_g)
    cots = (slot_w_b[:, :, None] * g_rows.astype(jnp.float32)).astype(jnp.bfloat16).reshape(-1, width)
    made_b = expert_backward(rows, cots, w_g, w_u, w_d).reshape(n_exp, cap, width)
    back_b = exchange_ep(made_b, "ep")

    places_f = slot_places(ids_fwd[0], n_exp, cap)
    picked_f = combine_rows(places_f, back_f.reshape(-1, width), top)
    mixed = jnp.sum(weights_f[:, :, None] * picked_f, axis=1)
    layer_out = (xf + mixed).astype(jnp.bfloat16)[None]
    places_b = slot_places(ids_bwd[0], n_exp, cap)
    picked_b = combine_rows(places_b, back_b.reshape(-1, width), top)
    dnorm = jnp.sum(picked_b, axis=1)
    input_grad = (grad.astype(jnp.float32) + norm_backward(xb, scale_b, gain, dnorm)).astype(
        jnp.bfloat16
    )[None]
    fwd_next = from_behind(layer_out, "pipe", 1)
    bwd_prev = from_behind(input_grad, "pipe", -1)
    return (fwd_next, bwd_prev)


def solution(mesh):
    placed = (
        P("pipe", "ep", None),
        P("pipe", "ep", None),
        P("pipe", "ep", None),
        P("pipe", "ep", None),
        P("pipe", "ep", None),
        P("pipe", "ep", None),
        P("pipe", "ep", None),
        P("pipe", None),
        P("pipe", "ep", None, None),
        P("pipe", "ep", None, None),
        P("pipe", "ep", None, None),
    )
    return jax.shard_map(
        local,
        mesh=mesh,
        in_specs=placed,
        out_specs=(P("pipe", "ep", None), P("pipe", "ep", None)),
        check_vma=False,
    )
```

```python
import jax
import jax.numpy as jnp
from jax import lax
from jax.sharding import PartitionSpec as P

EPS = 1e-06


def from_behind(block, axis, distance):
    devices = range(lax.axis_size(axis))
    route = [((i - distance) % len(devices), i) for i in devices]
    return lax.ppermute(block, axis, route)


def slot_places(ids, n_exp, cap):
    flat = ids.reshape(-1)
    onehot = (flat[:, None] == jnp.arange(n_exp, dtype=jnp.int32)[None, :]).astype(jnp.int32)
    before = jnp.cumsum(onehot, axis=0) - onehot
    slot = jnp.sum(before * onehot, axis=1)
    return flat * cap + slot


def rms_stats(x):
    xf = x.astype(jnp.float32)
    scale = lax.rsqrt(jnp.mean(xf * xf, axis=-1, keepdims=True) + EPS)
    return (xf, scale)


def expert_forward(rows, w_g, w_u, w_d):
    gate = jnp.dot(rows, w_g, preferred_element_type=jnp.float32)
    upper = jnp.dot(rows, w_u, preferred_element_type=jnp.float32)
    act = (jax.nn.silu(gate) * upper).astype(jnp.bfloat16)
    return jnp.dot(act, w_d, preferred_element_type=jnp.float32).astype(jnp.bfloat16)


def expert_backward(rows, cot, w_g, w_u, w_d):
    gate = jnp.dot(rows, w_g, preferred_element_type=jnp.float32)
    upper = jnp.dot(rows, w_u, preferred_element_type=jnp.float32)
    sigma = jax.nn.sigmoid(gate)
    dact = jnp.dot(cot, w_d.T, preferred_element_type=jnp.float32)
    dgate = (dact * upper * sigma * (1.0 + gate * (1.0 - sigma))).astype(jnp.bfloat16)
    dup = (dact * gate * sigma).astype(jnp.bfloat16)
    total = jnp.dot(dgate, w_g.T, preferred_element_type=jnp.float32) + jnp.dot(
        dup, w_u.T, preferred_element_type=jnp.float32
    )
    return total.astype(jnp.bfloat16)


def norm_backward(xf, scale, gain, upstream):
    scaled = gain * upstream
    inner = jnp.mean(xf * scaled, axis=-1, keepdims=True)
    return scale * scaled - xf * (scale * scale * scale) * inner


def expert_slots(ids_all, weights_all, me, cap):
    match = ids_all == me
    chosen = jnp.any(match, axis=-1)
    weight = jnp.sum(jnp.where(match, weights_all, 0.0), axis=-1)
    pos = jnp.cumsum(chosen.astype(jnp.int32), axis=1) - chosen.astype(jnp.int32)
    slot = jnp.arange(cap, dtype=jnp.int32)[None, :, None]
    onehot = chosen[:, None, :] & (pos[:, None, :] == slot)
    slot_w = jnp.sum(jnp.where(onehot, weight[:, None, :], 0.0), axis=-1)
    return onehot.astype(jnp.bfloat16), slot_w


def pick_rows(onehot, rows):
    picked = jnp.einsum("bct,btd->bcd", onehot, rows, preferred_element_type=jnp.float32)
    return picked.astype(jnp.bfloat16)


def combine_rows(places, back, top):
    count = back.shape[0]
    onehot = (places[:, None] == jnp.arange(count, dtype=jnp.int32)[None, :]).astype(jnp.bfloat16)
    picked = jnp.dot(onehot, back, preferred_element_type=jnp.float32)
    return picked.reshape(-1, top, back.shape[1])


def _pairs(n, n2, stage, move):
    out = []
    for i in range(n):
        e1, e2 = i // n2, i % n2
        if stage == 1:
            e1 = move(e1)
        else:
            e2 = move(e2)
        out.append((i, e1 * n2 + e2))
    return out


def gather_ep(v, axis_name):
    n = lax.axis_size(axis_name)
    n2 = 4
    if n % n2 or v.shape[0] % 2:
        return lax.all_gather(v, axis_name, axis=0, tiled=False)
    n1 = n // n2
    me = lax.axis_index(axis_name)
    e1, e2 = me // n2, me % n2
    s1 = jnp.zeros((n1,) + v.shape, v.dtype)
    s1 = lax.dynamic_update_index_in_dim(s1, v, e1, 0)
    for d in range(1, n1):
        got = lax.ppermute(v, axis_name, _pairs(n, n2, 1, lambda a: (a + d) % n1))
        s1 = lax.dynamic_update_index_in_dim(s1, got, (e1 - d) % n1, 0)
    flip_x = lambda a: a ^ 1
    flip_y = lambda a: a ^ 2
    px = lax.ppermute(s1, axis_name, _pairs(n, n2, 2, flip_x))
    py = lax.ppermute(s1, axis_name, _pairs(n, n2, 2, flip_y))
    h = v.shape[0] // 2
    d1 = lax.ppermute(px[:, :h], axis_name, _pairs(n, n2, 2, flip_y))
    d2 = lax.ppermute(py[:, h:], axis_name, _pairs(n, n2, 2, flip_x))
    diag = jnp.concatenate([d1, d2], axis=1)
    s2 = jnp.zeros((n2,) + s1.shape, v.dtype)
    s2 = lax.dynamic_update_index_in_dim(s2, s1, e2, 0)
    s2 = lax.dynamic_update_index_in_dim(s2, px, e2 ^ 1, 0)
    s2 = lax.dynamic_update_index_in_dim(s2, py, e2 ^ 2, 0)
    s2 = lax.dynamic_update_index_in_dim(s2, diag, e2 ^ 3, 0)
    return jnp.swapaxes(s2, 0, 1).reshape((n,) + v.shape)


def exchange_ep(blocks, axis_name):
    n = lax.axis_size(axis_name)
    me = lax.axis_index(axis_name)
    out = lax.dynamic_update_index_in_dim(
        jnp.zeros_like(blocks), lax.dynamic_index_in_dim(blocks, me, 0, keepdims=False), me, 0
    )
    for d in range(1, n):
        part = lax.dynamic_index_in_dim(blocks, (me + d) % n, 0, keepdims=False)
        got = lax.ppermute(part, axis_name, [(i, (i + d) % n) for i in range(n)])
        out = lax.dynamic_update_index_in_dim(out, got, (me - d) % n, 0)
    return out


def local(
    x_fwd, ids_fwd, route_fwd, x_bwd, grad_bwd, ids_bwd, route_bwd, norm_gain, w_gate, w_up, w_down
):
    n_exp = lax.axis_size("ep")
    me = lax.axis_index("ep")
    tok_dev = x_fwd.shape[1]
    width = x_fwd.shape[2]
    top = ids_fwd.shape[2]
    cap = 3 * tok_dev * top // (2 * n_exp)
    gain = norm_gain[0].astype(jnp.float32)
    w_g = w_gate[0, 0]
    w_u = w_up[0, 0]
    w_d = w_down[0, 0]
    xf, scale_f = rms_stats(x_fwd[0])
    h_f = (xf * scale_f * gain).astype(jnp.bfloat16)
    xb, scale_b = rms_stats(x_bwd[0])
    h_b = (xb * scale_b * gain).astype(jnp.bfloat16)
    grad = grad_bwd[0]
    weights_f = route_fwd[0] / jnp.sum(route_fwd[0], axis=-1, keepdims=True)
    weights_b = route_bwd[0] / jnp.sum(route_bwd[0], axis=-1, keepdims=True)

    def split3(r):
        hi = lax.reduce_precision(r, exponent_bits=8, mantissa_bits=7)
        rest = r - hi
        mid = lax.reduce_precision(rest, exponent_bits=8, mantissa_bits=7)
        return jnp.concatenate([hi, mid, rest - mid], axis=-1).astype(jnp.bfloat16)

    def join3(p):
        p = p.astype(jnp.float32)
        return (p[..., 0:top] + p[..., top:2 * top]) + p[..., 2 * top:3 * top]

    def padded(parts):
        v = jnp.concatenate(parts, axis=-1)
        pad = (-v.shape[-1]) % 128
        return jnp.concatenate([v, jnp.zeros((tok_dev, pad), v.dtype)], axis=-1)

    meta_f = padded([ids_fwd[0].astype(jnp.bfloat16), split3(route_fwd[0])])
    meta_b = padded([ids_bwd[0].astype(jnp.bfloat16), split3(route_bwd[0])])
    message_f = gather_ep(jnp.concatenate([h_f, meta_f], axis=-1), "ep")
    all_h_f = message_f[..., 0:width]
    got = message_f[..., width:]
    all_ids_f = got[..., 0:top].astype(jnp.int32)
    all_route_f = join3(got[..., top:4 * top])

    onehot_f, _ = expert_slots(all_ids_f, all_route_f, me, cap)
    rows = pick_rows(onehot_f, all_h_f).reshape(-1, width)
    made_f = expert_forward(rows, w_g, w_u, w_d).reshape(n_exp, cap, width)
    made_f, message_b = lax.optimization_barrier((made_f, jnp.concatenate([h_b, grad, meta_b], axis=-1)))
    back_f = exchange_ep(made_f, "ep")
    message_b = gather_ep(message_b, "ep")
    all_h_b = message_b[..., 0:width]
    all_g = message_b[..., width:2 * width]
    got = message_b[..., 2 * width:]
    all_ids_b = got[..., 0:top].astype(jnp.int32)
    all_route_b = join3(got[..., top:4 * top])
    all_w_b = all_route_b / jnp.sum(all_route_b, axis=-1, keepdims=True)

    onehot_b, slot_w_b = expert_slots(all_ids_b, all_w_b, me, cap)
    rows = pick_rows(onehot_b, all_h_b).reshape(-1, width)
    g_rows = pick_rows(onehot_b, all_g)
    cots = (slot_w_b[:, :, None] * g_rows.astype(jnp.float32)).astype(jnp.bfloat16).reshape(-1, width)
    made_b = expert_backward(rows, cots, w_g, w_u, w_d).reshape(n_exp, cap, width)
    back_b = exchange_ep(made_b, "ep")

    places_f = slot_places(ids_fwd[0], n_exp, cap)
    picked_f = combine_rows(places_f, back_f.reshape(-1, width), top)
    mixed = jnp.sum(weights_f[:, :, None] * picked_f, axis=1)
    layer_out = (xf + mixed).astype(jnp.bfloat16)[None]
    places_b = slot_places(ids_bwd[0], n_exp, cap)
    picked_b = combine_rows(places_b, back_b.reshape(-1, width), top)
    dnorm = jnp.sum(picked_b, axis=1)
    input_grad = (grad.astype(jnp.float32) + norm_backward(xb, scale_b, gain, dnorm)).astype(
        jnp.bfloat16
    )[None]
    fwd_next = from_behind(layer_out, "pipe", 1)
    bwd_prev = from_behind(input_grad, "pipe", -1)
    return (fwd_next, bwd_prev)


def solution(mesh):
    placed = (
        P("pipe", "ep", None),
        P("pipe", "ep", None),
        P("pipe", "ep", None),
        P("pipe", "ep", None),
        P("pipe", "ep", None),
        P("pipe", "ep", None),
        P("pipe", "ep", None),
        P("pipe", None),
        P("pipe", "ep", None, None),
        P("pipe", "ep", None, None),
        P("pipe", "ep", None, None),
    )
    return jax.shard_map(
        local,
        mesh=mesh,
        in_specs=placed,
        out_specs=(P("pipe", "ep", None), P("pipe", "ep", None)),
        check_vma=False,
    )
```

```python
import jax
import jax.numpy as jnp
from jax import lax
from jax.sharding import PartitionSpec as P

EPS = 1e-06


def from_behind(block, axis, distance):
    devices = range(lax.axis_size(axis))
    route = [((i - distance) % len(devices), i) for i in devices]
    return lax.ppermute(block, axis, route)


def slot_places(ids, n_exp, cap):
    flat = ids.reshape(-1)
    onehot = (flat[:, None] == jnp.arange(n_exp, dtype=jnp.int32)[None, :]).astype(jnp.int32)
    before = jnp.cumsum(onehot, axis=0) - onehot
    slot = jnp.sum(before * onehot, axis=1)
    return flat * cap + slot


def rms_stats(x):
    xf = x.astype(jnp.float32)
    scale = lax.rsqrt(jnp.mean(xf * xf, axis=-1, keepdims=True) + EPS)
    return (xf, scale)


def expert_forward(rows, w_g, w_u, w_d):
    gate = jnp.dot(rows, w_g, preferred_element_type=jnp.float32)
    upper = jnp.dot(rows, w_u, preferred_element_type=jnp.float32)
    act = (jax.nn.silu(gate) * upper).astype(jnp.bfloat16)
    return jnp.dot(act, w_d, preferred_element_type=jnp.float32).astype(jnp.bfloat16)


def expert_backward(rows, cot, w_g, w_u, w_d):
    gate = jnp.dot(rows, w_g, preferred_element_type=jnp.float32)
    upper = jnp.dot(rows, w_u, preferred_element_type=jnp.float32)
    sigma = jax.nn.sigmoid(gate)
    dact = jnp.dot(cot, w_d.T, preferred_element_type=jnp.float32)
    dgate = (dact * upper * sigma * (1.0 + gate * (1.0 - sigma))).astype(jnp.bfloat16)
    dup = (dact * gate * sigma).astype(jnp.bfloat16)
    total = jnp.dot(dgate, w_g.T, preferred_element_type=jnp.float32) + jnp.dot(
        dup, w_u.T, preferred_element_type=jnp.float32
    )
    return total.astype(jnp.bfloat16)


def norm_backward(xf, scale, gain, upstream):
    scaled = gain * upstream
    inner = jnp.mean(xf * scaled, axis=-1, keepdims=True)
    return scale * scaled - xf * (scale * scale * scale) * inner


def expert_slots(ids_all, weights_all, me, cap):
    match = ids_all == me
    chosen = jnp.any(match, axis=-1)
    weight = jnp.sum(jnp.where(match, weights_all, 0.0), axis=-1)
    pos = jnp.cumsum(chosen.astype(jnp.int32), axis=1) - chosen.astype(jnp.int32)
    slot = jnp.arange(cap, dtype=jnp.int32)[None, :, None]
    onehot = chosen[:, None, :] & (pos[:, None, :] == slot)
    slot_w = jnp.sum(jnp.where(onehot, weight[:, None, :], 0.0), axis=-1)
    return onehot.astype(jnp.bfloat16), slot_w


def pick_rows(onehot, rows):
    picked = jnp.einsum("bct,btd->bcd", onehot, rows, preferred_element_type=jnp.float32)
    return picked.astype(jnp.bfloat16)


def combine_rows(places, back, top):
    count = back.shape[0]
    onehot = (places[:, None] == jnp.arange(count, dtype=jnp.int32)[None, :]).astype(jnp.bfloat16)
    picked = jnp.dot(onehot, back, preferred_element_type=jnp.float32)
    return picked.reshape(-1, top, back.shape[1])


def _pairs(n, n2, stage, move):
    out = []
    for i in range(n):
        e1, e2 = i // n2, i % n2
        if stage == 1:
            e1 = move(e1)
        else:
            e2 = move(e2)
        out.append((i, e1 * n2 + e2))
    return out


def gather_ep(v, axis_name):
    n = lax.axis_size(axis_name)
    n2 = 4
    if n % n2 or v.shape[0] % 4:
        return lax.all_gather(v, axis_name, axis=0, tiled=False)
    n1 = n // n2
    me = lax.axis_index(axis_name)
    e1, e2 = me // n2, me % n2

    def along(part):
        s1 = jnp.zeros((n1,) + part.shape, part.dtype)
        s1 = lax.dynamic_update_index_in_dim(s1, part, e1, 0)
        for d in range(1, n1):
            got = lax.ppermute(part, axis_name, _pairs(n, n2, 1, lambda a: (a + d) % n1))
            s1 = lax.dynamic_update_index_in_dim(s1, got, (e1 - d) % n1, 0)
        return s1

    def across(s1):
        flip_x = lambda a: a ^ 1
        flip_y = lambda a: a ^ 2
        px = lax.ppermute(s1, axis_name, _pairs(n, n2, 2, flip_x))
        py = lax.ppermute(s1, axis_name, _pairs(n, n2, 2, flip_y))
        h = s1.shape[1] // 2
        d1 = lax.ppermute(px[:, :h], axis_name, _pairs(n, n2, 2, flip_y))
        d2 = lax.ppermute(py[:, h:], axis_name, _pairs(n, n2, 2, flip_x))
        diag = jnp.concatenate([d1, d2], axis=1)
        s2 = jnp.zeros((n2,) + s1.shape, s1.dtype)
        s2 = lax.dynamic_update_index_in_dim(s2, s1, e2, 0)
        s2 = lax.dynamic_update_index_in_dim(s2, px, e2 ^ 1, 0)
        s2 = lax.dynamic_update_index_in_dim(s2, py, e2 ^ 2, 0)
        s2 = lax.dynamic_update_index_in_dim(s2, diag, e2 ^ 3, 0)
        return jnp.swapaxes(s2, 0, 1).reshape((n,) + s1.shape[1:])

    half = v.shape[0] // 2
    first = along(v[:half])
    first, rest = lax.optimization_barrier((first, v[half:]))
    second = along(rest)
    return jnp.concatenate([across(first), across(second)], axis=1)

def local(
    x_fwd, ids_fwd, route_fwd, x_bwd, grad_bwd, ids_bwd, route_bwd, norm_gain, w_gate, w_up, w_down
):
    n_exp = lax.axis_size("ep")
    me = lax.axis_index("ep")
    tok_dev = x_fwd.shape[1]
    width = x_fwd.shape[2]
    top = ids_fwd.shape[2]
    cap = 3 * tok_dev * top // (2 * n_exp)
    gain = norm_gain[0].astype(jnp.float32)
    w_g = w_gate[0, 0]
    w_u = w_up[0, 0]
    w_d = w_down[0, 0]
    xf, scale_f = rms_stats(x_fwd[0])
    h_f = (xf * scale_f * gain).astype(jnp.bfloat16)
    xb, scale_b = rms_stats(x_bwd[0])
    h_b = (xb * scale_b * gain).astype(jnp.bfloat16)
    grad = grad_bwd[0]
    weights_f = route_fwd[0] / jnp.sum(route_fwd[0], axis=-1, keepdims=True)
    weights_b = route_bwd[0] / jnp.sum(route_bwd[0], axis=-1, keepdims=True)

    def split3(r):
        hi = lax.reduce_precision(r, exponent_bits=8, mantissa_bits=7)
        rest = r - hi
        mid = lax.reduce_precision(rest, exponent_bits=8, mantissa_bits=7)
        return jnp.concatenate([hi, mid, rest - mid], axis=-1).astype(jnp.bfloat16)

    def join3(p):
        p = p.astype(jnp.float32)
        return (p[..., 0:top] + p[..., top:2 * top]) + p[..., 2 * top:3 * top]

    meta = jnp.concatenate(
        [ids_fwd[0].astype(jnp.bfloat16), ids_bwd[0].astype(jnp.bfloat16), split3(route_fwd[0]), split3(route_bwd[0])],
        axis=-1,
    )
    pad = (-meta.shape[-1]) % 128
    meta = jnp.concatenate([meta, jnp.zeros((tok_dev, pad), jnp.bfloat16)], axis=-1)
    message = gather_ep(jnp.concatenate([h_f, h_b, grad, meta], axis=-1), "ep")
    all_h_f = message[..., 0:width]
    all_h_b = message[..., width:2 * width]
    all_g = message[..., 2 * width:3 * width]
    got = message[..., 3 * width:]
    all_ids_f = got[..., 0:top].astype(jnp.int32)
    all_ids_b = got[..., top:2 * top].astype(jnp.int32)
    all_route_f = join3(got[..., 2 * top:5 * top])
    all_route_b = join3(got[..., 5 * top:8 * top])
    all_w_f = all_route_f / jnp.sum(all_route_f, axis=-1, keepdims=True)
    all_w_b = all_route_b / jnp.sum(all_route_b, axis=-1, keepdims=True)

    onehot_f, _ = expert_slots(all_ids_f, all_w_f, me, cap)
    rows = pick_rows(onehot_f, all_h_f).reshape(-1, width)
    made_f = expert_forward(rows, w_g, w_u, w_d).reshape(n_exp, cap, width)
    back_f = lax.all_to_all(made_f, "ep", split_axis=0, concat_axis=0, tiled=True)

    onehot_b, slot_w_b = expert_slots(all_ids_b, all_w_b, me, cap)
    rows = pick_rows(onehot_b, all_h_b).reshape(-1, width)
    g_rows = pick_rows(onehot_b, all_g)
    cots = (slot_w_b[:, :, None] * g_rows.astype(jnp.float32)).astype(jnp.bfloat16).reshape(-1, width)
    made_b = expert_backward(rows, cots, w_g, w_u, w_d).reshape(n_exp, cap, width)
    back_b = lax.all_to_all(made_b, "ep", split_axis=0, concat_axis=0, tiled=True)

    places_f = slot_places(ids_fwd[0], n_exp, cap)
    picked_f = combine_rows(places_f, back_f.reshape(-1, width), top)
    mixed = jnp.sum(weights_f[:, :, None] * picked_f, axis=1)
    layer_out = (xf + mixed).astype(jnp.bfloat16)[None]
    places_b = slot_places(ids_bwd[0], n_exp, cap)
    picked_b = combine_rows(places_b, back_b.reshape(-1, width), top)
    dnorm = jnp.sum(picked_b, axis=1)
    input_grad = (grad.astype(jnp.float32) + norm_backward(xb, scale_b, gain, dnorm)).astype(
        jnp.bfloat16
    )[None]
    fwd_next = from_behind(layer_out, "pipe", 1)
    bwd_prev = from_behind(input_grad, "pipe", -1)
    return (fwd_next, bwd_prev)


def solution(mesh):
    placed = (
        P("pipe", "ep", None),
        P("pipe", "ep", None),
        P("pipe", "ep", None),
        P("pipe", "ep", None),
        P("pipe", "ep", None),
        P("pipe", "ep", None),
        P("pipe", "ep", None),
        P("pipe", None),
        P("pipe", "ep", None, None),
        P("pipe", "ep", None, None),
        P("pipe", "ep", None, None),
    )
    return jax.shard_map(
        local,
        mesh=mesh,
        in_specs=placed,
        out_specs=(P("pipe", "ep", None), P("pipe", "ep", None)),
        check_vma=False,
    )
```

```python
import jax
import jax.numpy as jnp
from jax import lax
from jax.sharding import PartitionSpec as P

EPS = 1e-06
CHUNKS = 4


def from_behind(block, axis, distance):
    devices = range(lax.axis_size(axis))
    route = [((i - distance) % len(devices), i) for i in devices]
    return lax.ppermute(block, axis, route)


def slot_places(ids, n_exp, cap):
    flat = ids.reshape(-1)
    onehot = (flat[:, None] == jnp.arange(n_exp, dtype=jnp.int32)[None, :]).astype(jnp.int32)
    before = jnp.cumsum(onehot, axis=0) - onehot
    slot = jnp.sum(before * onehot, axis=1)
    return flat * cap + slot


def rms_stats(x):
    xf = x.astype(jnp.float32)
    scale = lax.rsqrt(jnp.mean(xf * xf, axis=-1, keepdims=True) + EPS)
    return (xf, scale)


def expert_forward(rows, w_g, w_u, w_d):
    gate = jnp.dot(rows, w_g, preferred_element_type=jnp.float32)
    upper = jnp.dot(rows, w_u, preferred_element_type=jnp.float32)
    act = (jax.nn.silu(gate) * upper).astype(jnp.bfloat16)
    return jnp.dot(act, w_d, preferred_element_type=jnp.float32).astype(jnp.bfloat16)


def expert_backward(rows, cot, w_g, w_u, w_d):
    gate = jnp.dot(rows, w_g, preferred_element_type=jnp.float32)
    upper = jnp.dot(rows, w_u, preferred_element_type=jnp.float32)
    sigma = jax.nn.sigmoid(gate)
    dact = jnp.dot(cot, w_d.T, preferred_element_type=jnp.float32)
    dgate = (dact * upper * sigma * (1.0 + gate * (1.0 - sigma))).astype(jnp.bfloat16)
    dup = (dact * gate * sigma).astype(jnp.bfloat16)
    total = jnp.dot(dgate, w_g.T, preferred_element_type=jnp.float32) + jnp.dot(
        dup, w_u.T, preferred_element_type=jnp.float32
    )
    return total.astype(jnp.bfloat16)


def norm_backward(xf, scale, gain, upstream):
    scaled = gain * upstream
    inner = jnp.mean(xf * scaled, axis=-1, keepdims=True)
    return scale * scaled - xf * (scale * scale * scale) * inner


def expert_slots(ids_all, weights_all, me, cap):
    match = ids_all == me
    chosen = jnp.any(match, axis=-1)
    weight = jnp.sum(jnp.where(match, weights_all, 0.0), axis=-1)
    pos = jnp.cumsum(chosen.astype(jnp.int32), axis=1) - chosen.astype(jnp.int32)
    slot = jnp.arange(cap, dtype=jnp.int32)[None, :, None]
    onehot = chosen[:, None, :] & (pos[:, None, :] == slot)
    slot_w = jnp.sum(jnp.where(onehot, weight[:, None, :], 0.0), axis=-1)
    return onehot.astype(jnp.bfloat16), slot_w


def pick_rows(onehot, rows):
    picked = jnp.einsum("bct,btd->bcd", onehot, rows, preferred_element_type=jnp.float32)
    return picked.astype(jnp.bfloat16)


def combine_rows(places, back, top):
    count = back.shape[0]
    onehot = (places[:, None] == jnp.arange(count, dtype=jnp.int32)[None, :]).astype(jnp.bfloat16)
    picked = jnp.dot(onehot, back, preferred_element_type=jnp.float32)
    return picked.reshape(-1, top, back.shape[1])


def _pairs(n, n2, stage, move):
    out = []
    for i in range(n):
        e1, e2 = i // n2, i % n2
        if stage == 1:
            e1 = move(e1)
        else:
            e2 = move(e2)
        out.append((i, e1 * n2 + e2))
    return out


def gather_ep(v, axis_name):
    n = lax.axis_size(axis_name)
    n2 = 4
    if n % n2 or v.shape[0] % CHUNKS or v.shape[-1] % 128:
        return lax.all_gather(v, axis_name, axis=0, tiled=False)
    n1 = n // n2
    me = lax.axis_index(axis_name)
    e1, e2 = me // n2, me % n2

    def along(part):
        s1 = jnp.zeros((n1,) + part.shape, part.dtype)
        s1 = lax.dynamic_update_index_in_dim(s1, part, e1, 0)
        for d in range(1, n1):
            got = lax.ppermute(part, axis_name, _pairs(n, n2, 1, lambda a: (a + d) % n1))
            s1 = lax.dynamic_update_index_in_dim(s1, got, (e1 - d) % n1, 0)
        return s1

    def across(s1):
        flip_x = lambda a: a ^ 1
        flip_y = lambda a: a ^ 2
        px = lax.ppermute(s1, axis_name, _pairs(n, n2, 2, flip_x))
        py = lax.ppermute(s1, axis_name, _pairs(n, n2, 2, flip_y))
        h = (s1.shape[-1] // 256) * 128
        d1 = lax.ppermute(px[..., :h], axis_name, _pairs(n, n2, 2, flip_y))
        d2 = lax.ppermute(py[..., h:], axis_name, _pairs(n, n2, 2, flip_x))
        diag = jnp.concatenate([d1, d2], axis=-1)
        s2 = jnp.zeros((n2,) + s1.shape, s1.dtype)
        s2 = lax.dynamic_update_index_in_dim(s2, s1, e2, 0)
        s2 = lax.dynamic_update_index_in_dim(s2, px, e2 ^ 1, 0)
        s2 = lax.dynamic_update_index_in_dim(s2, py, e2 ^ 2, 0)
        s2 = lax.dynamic_update_index_in_dim(s2, diag, e2 ^ 3, 0)
        return jnp.swapaxes(s2, 0, 1).reshape((n,) + s1.shape[1:])

    step = v.shape[0] // CHUNKS
    done = []
    ready = along(v[:step])
    for c in range(1, CHUNKS):
        ready, part = lax.optimization_barrier((ready, v[c * step:(c + 1) * step]))
        done.append(across(ready))
        ready = along(part)
    done.append(across(ready))
    return jnp.concatenate(done, axis=1)

def local(
    x_fwd, ids_fwd, route_fwd, x_bwd, grad_bwd, ids_bwd, route_bwd, norm_gain, w_gate, w_up, w_down
):
    n_exp = lax.axis_size("ep")
    me = lax.axis_index("ep")
    tok_dev = x_fwd.shape[1]
    width = x_fwd.shape[2]
    top = ids_fwd.shape[2]
    cap = 3 * tok_dev * top // (2 * n_exp)
    gain = norm_gain[0].astype(jnp.float32)
    w_g = w_gate[0, 0]
    w_u = w_up[0, 0]
    w_d = w_down[0, 0]
    xf, scale_f = rms_stats(x_fwd[0])
    h_f = (xf * scale_f * gain).astype(jnp.bfloat16)
    xb, scale_b = rms_stats(x_bwd[0])
    h_b = (xb * scale_b * gain).astype(jnp.bfloat16)
    grad = grad_bwd[0]
    weights_f = route_fwd[0] / jnp.sum(route_fwd[0], axis=-1, keepdims=True)
    weights_b = route_bwd[0] / jnp.sum(route_bwd[0], axis=-1, keepdims=True)

    def split3(r):
        hi = lax.reduce_precision(r, exponent_bits=8, mantissa_bits=7)
        rest = r - hi
        mid = lax.reduce_precision(rest, exponent_bits=8, mantissa_bits=7)
        return jnp.concatenate([hi, mid, rest - mid], axis=-1).astype(jnp.bfloat16)

    def join3(p):
        p = p.astype(jnp.float32)
        return (p[..., 0:top] + p[..., top:2 * top]) + p[..., 2 * top:3 * top]

    meta = jnp.concatenate(
        [ids_fwd[0].astype(jnp.bfloat16), ids_bwd[0].astype(jnp.bfloat16), split3(route_fwd[0]), split3(route_bwd[0])],
        axis=-1,
    )
    pad = (-meta.shape[-1]) % 128
    meta = jnp.concatenate([meta, jnp.zeros((tok_dev, pad), jnp.bfloat16)], axis=-1)
    message = gather_ep(jnp.concatenate([h_f, h_b, grad, meta], axis=-1), "ep")
    all_h_f = message[..., 0:width]
    all_h_b = message[..., width:2 * width]
    all_g = message[..., 2 * width:3 * width]
    got = message[..., 3 * width:]
    all_ids_f = got[..., 0:top].astype(jnp.int32)
    all_ids_b = got[..., top:2 * top].astype(jnp.int32)
    all_route_f = join3(got[..., 2 * top:5 * top])
    all_route_b = join3(got[..., 5 * top:8 * top])
    all_w_f = all_route_f / jnp.sum(all_route_f, axis=-1, keepdims=True)
    all_w_b = all_route_b / jnp.sum(all_route_b, axis=-1, keepdims=True)

    onehot_f, _ = expert_slots(all_ids_f, all_w_f, me, cap)
    rows = pick_rows(onehot_f, all_h_f).reshape(-1, width)
    made_f = expert_forward(rows, w_g, w_u, w_d).reshape(n_exp, cap, width)
    back_f = lax.all_to_all(made_f, "ep", split_axis=0, concat_axis=0, tiled=True)

    onehot_b, slot_w_b = expert_slots(all_ids_b, all_w_b, me, cap)
    rows = pick_rows(onehot_b, all_h_b).reshape(-1, width)
    g_rows = pick_rows(onehot_b, all_g)
    cots = (slot_w_b[:, :, None] * g_rows.astype(jnp.float32)).astype(jnp.bfloat16).reshape(-1, width)
    made_b = expert_backward(rows, cots, w_g, w_u, w_d).reshape(n_exp, cap, width)
    back_b = lax.all_to_all(made_b, "ep", split_axis=0, concat_axis=0, tiled=True)

    places_f = slot_places(ids_fwd[0], n_exp, cap)
    picked_f = combine_rows(places_f, back_f.reshape(-1, width), top)
    mixed = jnp.sum(weights_f[:, :, None] * picked_f, axis=1)
    layer_out = (xf + mixed).astype(jnp.bfloat16)[None]
    places_b = slot_places(ids_bwd[0], n_exp, cap)
    picked_b = combine_rows(places_b, back_b.reshape(-1, width), top)
    dnorm = jnp.sum(picked_b, axis=1)
    input_grad = (grad.astype(jnp.float32) + norm_backward(xb, scale_b, gain, dnorm)).astype(
        jnp.bfloat16
    )[None]
    fwd_next = from_behind(layer_out, "pipe", 1)
    bwd_prev = from_behind(input_grad, "pipe", -1)
    return (fwd_next, bwd_prev)


def solution(mesh):
    placed = (
        P("pipe", "ep", None),
        P("pipe", "ep", None),
        P("pipe", "ep", None),
        P("pipe", "ep", None),
        P("pipe", "ep", None),
        P("pipe", "ep", None),
        P("pipe", "ep", None),
        P("pipe", None),
        P("pipe", "ep", None, None),
        P("pipe", "ep", None, None),
        P("pipe", "ep", None, None),
    )
    return jax.shard_map(
        local,
        mesh=mesh,
        in_specs=placed,
        out_specs=(P("pipe", "ep", None), P("pipe", "ep", None)),
        check_vma=False,
    )
```

```python
import jax
import jax.numpy as jnp
from jax import lax
from jax.sharding import PartitionSpec as P

EPS = 1e-06


def from_behind(block, axis, distance):
    devices = range(lax.axis_size(axis))
    route = [((i - distance) % len(devices), i) for i in devices]
    return lax.ppermute(block, axis, route)


def slot_places(ids, n_exp, cap):
    flat = ids.reshape(-1)
    onehot = (flat[:, None] == jnp.arange(n_exp, dtype=jnp.int32)[None, :]).astype(jnp.int32)
    before = jnp.cumsum(onehot, axis=0) - onehot
    slot = jnp.sum(before * onehot, axis=1)
    return flat * cap + slot


def rms_stats(x):
    xf = x.astype(jnp.float32)
    scale = lax.rsqrt(jnp.mean(xf * xf, axis=-1, keepdims=True) + EPS)
    return (xf, scale)


def expert_forward(rows, w_g, w_u, w_d):
    gate = jnp.dot(rows, w_g, preferred_element_type=jnp.float32)
    upper = jnp.dot(rows, w_u, preferred_element_type=jnp.float32)
    act = (jax.nn.silu(gate) * upper).astype(jnp.bfloat16)
    return jnp.dot(act, w_d, preferred_element_type=jnp.float32).astype(jnp.bfloat16)


def expert_backward(rows, cot, w_g, w_u, w_d):
    gate = jnp.dot(rows, w_g, preferred_element_type=jnp.float32)
    upper = jnp.dot(rows, w_u, preferred_element_type=jnp.float32)
    sigma = jax.nn.sigmoid(gate)
    dact = jnp.dot(cot, w_d.T, preferred_element_type=jnp.float32)
    dgate = (dact * upper * sigma * (1.0 + gate * (1.0 - sigma))).astype(jnp.bfloat16)
    dup = (dact * gate * sigma).astype(jnp.bfloat16)
    total = jnp.dot(dgate, w_g.T, preferred_element_type=jnp.float32) + jnp.dot(
        dup, w_u.T, preferred_element_type=jnp.float32
    )
    return total.astype(jnp.bfloat16)


def norm_backward(xf, scale, gain, upstream):
    scaled = gain * upstream
    inner = jnp.mean(xf * scaled, axis=-1, keepdims=True)
    return scale * scaled - xf * (scale * scale * scale) * inner


def expert_slots(ids_all, weights_all, me, cap):
    match = ids_all == me
    chosen = jnp.any(match, axis=-1)
    weight = jnp.sum(jnp.where(match, weights_all, 0.0), axis=-1)
    pos = jnp.cumsum(chosen.astype(jnp.int32), axis=1) - chosen.astype(jnp.int32)
    slot = jnp.arange(cap, dtype=jnp.int32)[None, :, None]
    onehot = chosen[:, None, :] & (pos[:, None, :] == slot)
    slot_w = jnp.sum(jnp.where(onehot, weight[:, None, :], 0.0), axis=-1)
    return onehot.astype(jnp.bfloat16), slot_w


def pick_rows(onehot, rows):
    picked = jnp.einsum("bct,btd->bcd", onehot, rows, preferred_element_type=jnp.float32)
    return picked.astype(jnp.bfloat16)


def combine_rows(places, back, top):
    count = back.shape[0]
    onehot = (places[:, None] == jnp.arange(count, dtype=jnp.int32)[None, :]).astype(jnp.bfloat16)
    picked = jnp.dot(onehot, back, preferred_element_type=jnp.float32)
    return picked.reshape(-1, top, back.shape[1])


def _pairs(n, n2, stage, move):
    out = []
    for i in range(n):
        e1, e2 = i // n2, i % n2
        if stage == 1:
            e1 = move(e1)
        else:
            e2 = move(e2)
        out.append((i, e1 * n2 + e2))
    return out


def gather_chain(parts, axis_name):
    n = lax.axis_size(axis_name)
    n2 = 4
    if n % n2 or any(v.shape[-1] % 128 for v in parts):
        return [lax.all_gather(v, axis_name, axis=0, tiled=False) for v in parts]
    n1 = n // n2
    me = lax.axis_index(axis_name)
    e1, e2 = me // n2, me % n2

    def along(part):
        s1 = jnp.zeros((n1,) + part.shape, part.dtype)
        s1 = lax.dynamic_update_index_in_dim(s1, part, e1, 0)
        for d in range(1, n1):
            got = lax.ppermute(part, axis_name, _pairs(n, n2, 1, lambda a: (a + d) % n1))
            s1 = lax.dynamic_update_index_in_dim(s1, got, (e1 - d) % n1, 0)
        return s1

    def across(s1):
        flip_x = lambda a: a ^ 1
        flip_y = lambda a: a ^ 2
        px = lax.ppermute(s1, axis_name, _pairs(n, n2, 2, flip_x))
        py = lax.ppermute(s1, axis_name, _pairs(n, n2, 2, flip_y))
        h = (s1.shape[-1] // 256) * 128
        d1 = lax.ppermute(px[..., :h], axis_name, _pairs(n, n2, 2, flip_y))
        d2 = lax.ppermute(py[..., h:], axis_name, _pairs(n, n2, 2, flip_x))
        diag = jnp.concatenate([d1, d2], axis=-1)
        s2 = jnp.zeros((n2,) + s1.shape, s1.dtype)
        s2 = lax.dynamic_update_index_in_dim(s2, s1, e2, 0)
        s2 = lax.dynamic_update_index_in_dim(s2, px, e2 ^ 1, 0)
        s2 = lax.dynamic_update_index_in_dim(s2, py, e2 ^ 2, 0)
        s2 = lax.dynamic_update_index_in_dim(s2, diag, e2 ^ 3, 0)
        return jnp.swapaxes(s2, 0, 1).reshape((n,) + s1.shape[1:])

    done = []
    ready = along(parts[0])
    for part in parts[1:]:
        ready, part = lax.optimization_barrier((ready, part))
        done.append(across(ready))
        ready = along(part)
    done.append(across(ready))
    return done

def local(
    x_fwd, ids_fwd, route_fwd, x_bwd, grad_bwd, ids_bwd, route_bwd, norm_gain, w_gate, w_up, w_down
):
    n_exp = lax.axis_size("ep")
    me = lax.axis_index("ep")
    tok_dev = x_fwd.shape[1]
    width = x_fwd.shape[2]
    top = ids_fwd.shape[2]
    cap = 3 * tok_dev * top // (2 * n_exp)
    gain = norm_gain[0].astype(jnp.float32)
    w_g = w_gate[0, 0]
    w_u = w_up[0, 0]
    w_d = w_down[0, 0]
    xf, scale_f = rms_stats(x_fwd[0])
    h_f = (xf * scale_f * gain).astype(jnp.bfloat16)
    xb, scale_b = rms_stats(x_bwd[0])
    h_b = (xb * scale_b * gain).astype(jnp.bfloat16)
    grad = grad_bwd[0]
    weights_f = route_fwd[0] / jnp.sum(route_fwd[0], axis=-1, keepdims=True)
    weights_b = route_bwd[0] / jnp.sum(route_bwd[0], axis=-1, keepdims=True)

    def split3(r):
        hi = lax.reduce_precision(r, exponent_bits=8, mantissa_bits=7)
        rest = r - hi
        mid = lax.reduce_precision(rest, exponent_bits=8, mantissa_bits=7)
        return jnp.concatenate([hi, mid, rest - mid], axis=-1).astype(jnp.bfloat16)

    def join3(p):
        p = p.astype(jnp.float32)
        return (p[..., 0:top] + p[..., top:2 * top]) + p[..., 2 * top:3 * top]

    meta = jnp.concatenate(
        [ids_fwd[0].astype(jnp.bfloat16), ids_bwd[0].astype(jnp.bfloat16), split3(route_fwd[0]), split3(route_bwd[0])],
        axis=-1,
    )
    pad = (-meta.shape[-1]) % 128
    meta = jnp.concatenate([meta, jnp.zeros((tok_dev, pad), jnp.bfloat16)], axis=-1)
    message_f, message_b = gather_chain(
        [jnp.concatenate([h_f, meta], axis=-1), jnp.concatenate([h_b, grad], axis=-1)], "ep"
    )
    all_h_f = message_f[..., 0:width]
    got = message_f[..., width:]
    all_h_b = message_b[..., 0:width]
    all_g = message_b[..., width:2 * width]
    all_ids_f = got[..., 0:top].astype(jnp.int32)
    all_ids_b = got[..., top:2 * top].astype(jnp.int32)
    all_route_f = join3(got[..., 2 * top:5 * top])
    all_route_b = join3(got[..., 5 * top:8 * top])
    all_w_f = all_route_f / jnp.sum(all_route_f, axis=-1, keepdims=True)
    all_w_b = all_route_b / jnp.sum(all_route_b, axis=-1, keepdims=True)

    onehot_f, _ = expert_slots(all_ids_f, all_w_f, me, cap)
    rows = pick_rows(onehot_f, all_h_f).reshape(-1, width)
    made_f = expert_forward(rows, w_g, w_u, w_d).reshape(n_exp, cap, width)
    back_f = lax.all_to_all(made_f, "ep", split_axis=0, concat_axis=0, tiled=True)

    onehot_b, slot_w_b = expert_slots(all_ids_b, all_w_b, me, cap)
    rows = pick_rows(onehot_b, all_h_b).reshape(-1, width)
    g_rows = pick_rows(onehot_b, all_g)
    cots = (slot_w_b[:, :, None] * g_rows.astype(jnp.float32)).astype(jnp.bfloat16).reshape(-1, width)
    made_b = expert_backward(rows, cots, w_g, w_u, w_d).reshape(n_exp, cap, width)
    back_b = lax.all_to_all(made_b, "ep", split_axis=0, concat_axis=0, tiled=True)

    places_f = slot_places(ids_fwd[0], n_exp, cap)
    picked_f = combine_rows(places_f, back_f.reshape(-1, width), top)
    mixed = jnp.sum(weights_f[:, :, None] * picked_f, axis=1)
    layer_out = (xf + mixed).astype(jnp.bfloat16)[None]
    places_b = slot_places(ids_bwd[0], n_exp, cap)
    picked_b = combine_rows(places_b, back_b.reshape(-1, width), top)
    dnorm = jnp.sum(picked_b, axis=1)
    input_grad = (grad.astype(jnp.float32) + norm_backward(xb, scale_b, gain, dnorm)).astype(
        jnp.bfloat16
    )[None]
    fwd_next = from_behind(layer_out, "pipe", 1)
    bwd_prev = from_behind(input_grad, "pipe", -1)
    return (fwd_next, bwd_prev)


def solution(mesh):
    placed = (
        P("pipe", "ep", None),
        P("pipe", "ep", None),
        P("pipe", "ep", None),
        P("pipe", "ep", None),
        P("pipe", "ep", None),
        P("pipe", "ep", None),
        P("pipe", "ep", None),
        P("pipe", None),
        P("pipe", "ep", None, None),
        P("pipe", "ep", None, None),
        P("pipe", "ep", None, None),
    )
    return jax.shard_map(
        local,
        mesh=mesh,
        in_specs=placed,
        out_specs=(P("pipe", "ep", None), P("pipe", "ep", None)),
        check_vma=False,
    )
```

```python
import jax
import jax.numpy as jnp
from jax import lax
from jax.sharding import PartitionSpec as P

EPS = 1e-06


def from_behind(block, axis, distance):
    devices = range(lax.axis_size(axis))
    route = [((i - distance) % len(devices), i) for i in devices]
    return lax.ppermute(block, axis, route)


def slot_places(ids, n_exp, cap):
    flat = ids.reshape(-1)
    onehot = (flat[:, None] == jnp.arange(n_exp, dtype=jnp.int32)[None, :]).astype(jnp.int32)
    before = jnp.cumsum(onehot, axis=0) - onehot
    slot = jnp.sum(before * onehot, axis=1)
    return flat * cap + slot


def rms_stats(x):
    xf = x.astype(jnp.float32)
    scale = lax.rsqrt(jnp.mean(xf * xf, axis=-1, keepdims=True) + EPS)
    return (xf, scale)


def expert_forward(rows, w_g, w_u, w_d):
    gate = jnp.dot(rows, w_g, preferred_element_type=jnp.float32)
    upper = jnp.dot(rows, w_u, preferred_element_type=jnp.float32)
    act = (jax.nn.silu(gate) * upper).astype(jnp.bfloat16)
    return jnp.dot(act, w_d, preferred_element_type=jnp.float32).astype(jnp.bfloat16)


def expert_backward(rows, cot, w_g, w_u, w_d):
    gate = jnp.dot(rows, w_g, preferred_element_type=jnp.float32)
    upper = jnp.dot(rows, w_u, preferred_element_type=jnp.float32)
    sigma = jax.nn.sigmoid(gate)
    dact = jnp.dot(cot, w_d.T, preferred_element_type=jnp.float32)
    dgate = (dact * upper * sigma * (1.0 + gate * (1.0 - sigma))).astype(jnp.bfloat16)
    dup = (dact * gate * sigma).astype(jnp.bfloat16)
    total = jnp.dot(dgate, w_g.T, preferred_element_type=jnp.float32) + jnp.dot(
        dup, w_u.T, preferred_element_type=jnp.float32
    )
    return total.astype(jnp.bfloat16)


def norm_backward(xf, scale, gain, upstream):
    scaled = gain * upstream
    inner = jnp.mean(xf * scaled, axis=-1, keepdims=True)
    return scale * scaled - xf * (scale * scale * scale) * inner


def expert_slots(ids_all, weights_all, me, cap):
    match = ids_all == me
    chosen = jnp.any(match, axis=-1)
    weight = jnp.sum(jnp.where(match, weights_all, 0.0), axis=-1)
    pos = jnp.cumsum(chosen.astype(jnp.int32), axis=1) - chosen.astype(jnp.int32)
    slot = jnp.arange(cap, dtype=jnp.int32)[None, :, None]
    onehot = chosen[:, None, :] & (pos[:, None, :] == slot)
    slot_w = jnp.sum(jnp.where(onehot, weight[:, None, :], 0.0), axis=-1)
    return onehot.astype(jnp.bfloat16), slot_w


def pick_rows(onehot, rows):
    picked = jnp.einsum("bct,btd->bcd", onehot, rows, preferred_element_type=jnp.float32)
    return picked.astype(jnp.bfloat16)


def combine_rows(places, back, top):
    count = back.shape[0]
    onehot = (places[:, None] == jnp.arange(count, dtype=jnp.int32)[None, :]).astype(jnp.bfloat16)
    picked = jnp.dot(onehot, back, preferred_element_type=jnp.float32)
    return picked.reshape(-1, top, back.shape[1])


def _pairs(n, n2, stage, move):
    out = []
    for i in range(n):
        e1, e2 = i // n2, i % n2
        if stage == 1:
            e1 = move(e1)
        else:
            e2 = move(e2)
        out.append((i, e1 * n2 + e2))
    return out


def gather_chain(parts, axis_name):
    n = lax.axis_size(axis_name)
    n2 = 4
    if n % n2 or any(v.shape[-1] % 128 for v in parts):
        return [lax.all_gather(v, axis_name, axis=0, tiled=False) for v in parts]
    n1 = n // n2
    me = lax.axis_index(axis_name)
    e1, e2 = me // n2, me % n2

    def along(part):
        s1 = jnp.zeros((n1,) + part.shape, part.dtype)
        s1 = lax.dynamic_update_index_in_dim(s1, part, e1, 0)
        for d in range(1, n1):
            got = lax.ppermute(part, axis_name, _pairs(n, n2, 1, lambda a: (a + d) % n1))
            s1 = lax.dynamic_update_index_in_dim(s1, got, (e1 - d) % n1, 0)
        return s1

    def across(s1):
        flip_x = lambda a: a ^ 1
        flip_y = lambda a: a ^ 2
        px = lax.ppermute(s1, axis_name, _pairs(n, n2, 2, flip_x))
        py = lax.ppermute(s1, axis_name, _pairs(n, n2, 2, flip_y))
        h = (s1.shape[-1] // 256) * 128
        d1 = lax.ppermute(px[..., :h], axis_name, _pairs(n, n2, 2, flip_y))
        d2 = lax.ppermute(py[..., h:], axis_name, _pairs(n, n2, 2, flip_x))
        diag = jnp.concatenate([d1, d2], axis=-1)
        s2 = jnp.zeros((n2,) + s1.shape, s1.dtype)
        s2 = lax.dynamic_update_index_in_dim(s2, s1, e2, 0)
        s2 = lax.dynamic_update_index_in_dim(s2, px, e2 ^ 1, 0)
        s2 = lax.dynamic_update_index_in_dim(s2, py, e2 ^ 2, 0)
        s2 = lax.dynamic_update_index_in_dim(s2, diag, e2 ^ 3, 0)
        return jnp.swapaxes(s2, 0, 1).reshape((n,) + s1.shape[1:])

    done = []
    ready = along(parts[0])
    for part in parts[1:]:
        ready, part = lax.optimization_barrier((ready, part))
        done.append(across(ready))
        ready = along(part)
        done[-1], ready = lax.optimization_barrier((done[-1], ready))
    done.append(across(ready))
    return done

def local(
    x_fwd, ids_fwd, route_fwd, x_bwd, grad_bwd, ids_bwd, route_bwd, norm_gain, w_gate, w_up, w_down
):
    n_exp = lax.axis_size("ep")
    me = lax.axis_index("ep")
    tok_dev = x_fwd.shape[1]
    width = x_fwd.shape[2]
    top = ids_fwd.shape[2]
    cap = 3 * tok_dev * top // (2 * n_exp)
    gain = norm_gain[0].astype(jnp.float32)
    w_g = w_gate[0, 0]
    w_u = w_up[0, 0]
    w_d = w_down[0, 0]
    xf, scale_f = rms_stats(x_fwd[0])
    h_f = (xf * scale_f * gain).astype(jnp.bfloat16)
    xb, scale_b = rms_stats(x_bwd[0])
    h_b = (xb * scale_b * gain).astype(jnp.bfloat16)
    grad = grad_bwd[0]
    weights_f = route_fwd[0] / jnp.sum(route_fwd[0], axis=-1, keepdims=True)
    weights_b = route_bwd[0] / jnp.sum(route_bwd[0], axis=-1, keepdims=True)

    def split3(r):
        hi = lax.reduce_precision(r, exponent_bits=8, mantissa_bits=7)
        rest = r - hi
        mid = lax.reduce_precision(rest, exponent_bits=8, mantissa_bits=7)
        return jnp.concatenate([hi, mid, rest - mid], axis=-1).astype(jnp.bfloat16)

    def join3(p):
        p = p.astype(jnp.float32)
        return (p[..., 0:top] + p[..., top:2 * top]) + p[..., 2 * top:3 * top]

    meta = jnp.concatenate(
        [ids_fwd[0].astype(jnp.bfloat16), ids_bwd[0].astype(jnp.bfloat16), split3(route_fwd[0]), split3(route_bwd[0])],
        axis=-1,
    )
    pad = (-meta.shape[-1]) % 128
    meta = jnp.concatenate([meta, jnp.zeros((tok_dev, pad), jnp.bfloat16)], axis=-1)
    message_f, message_b = gather_chain(
        [jnp.concatenate([h_f, meta], axis=-1), jnp.concatenate([h_b, grad], axis=-1)], "ep"
    )
    all_h_f = message_f[..., 0:width]
    got = message_f[..., width:]
    all_h_b = message_b[..., 0:width]
    all_g = message_b[..., width:2 * width]
    all_ids_f = got[..., 0:top].astype(jnp.int32)
    all_ids_b = got[..., top:2 * top].astype(jnp.int32)
    all_route_f = join3(got[..., 2 * top:5 * top])
    all_route_b = join3(got[..., 5 * top:8 * top])
    all_w_f = all_route_f / jnp.sum(all_route_f, axis=-1, keepdims=True)
    all_w_b = all_route_b / jnp.sum(all_route_b, axis=-1, keepdims=True)

    onehot_f, _ = expert_slots(all_ids_f, all_w_f, me, cap)
    rows = pick_rows(onehot_f, all_h_f).reshape(-1, width)
    made_f = expert_forward(rows, w_g, w_u, w_d).reshape(n_exp, cap, width)
    back_f = lax.all_to_all(made_f, "ep", split_axis=0, concat_axis=0, tiled=True)

    onehot_b, slot_w_b = expert_slots(all_ids_b, all_w_b, me, cap)
    rows = pick_rows(onehot_b, all_h_b).reshape(-1, width)
    g_rows = pick_rows(onehot_b, all_g)
    cots = (slot_w_b[:, :, None] * g_rows.astype(jnp.float32)).astype(jnp.bfloat16).reshape(-1, width)
    made_b = expert_backward(rows, cots, w_g, w_u, w_d).reshape(n_exp, cap, width)
    back_b = lax.all_to_all(made_b, "ep", split_axis=0, concat_axis=0, tiled=True)

    places_f = slot_places(ids_fwd[0], n_exp, cap)
    picked_f = combine_rows(places_f, back_f.reshape(-1, width), top)
    mixed = jnp.sum(weights_f[:, :, None] * picked_f, axis=1)
    layer_out = (xf + mixed).astype(jnp.bfloat16)[None]
    places_b = slot_places(ids_bwd[0], n_exp, cap)
    picked_b = combine_rows(places_b, back_b.reshape(-1, width), top)
    dnorm = jnp.sum(picked_b, axis=1)
    input_grad = (grad.astype(jnp.float32) + norm_backward(xb, scale_b, gain, dnorm)).astype(
        jnp.bfloat16
    )[None]
    fwd_next = from_behind(layer_out, "pipe", 1)
    bwd_prev = from_behind(input_grad, "pipe", -1)
    return (fwd_next, bwd_prev)


def solution(mesh):
    placed = (
        P("pipe", "ep", None),
        P("pipe", "ep", None),
        P("pipe", "ep", None),
        P("pipe", "ep", None),
        P("pipe", "ep", None),
        P("pipe", "ep", None),
        P("pipe", "ep", None),
        P("pipe", None),
        P("pipe", "ep", None, None),
        P("pipe", "ep", None, None),
        P("pipe", "ep", None, None),
    )
    return jax.shard_map(
        local,
        mesh=mesh,
        in_specs=placed,
        out_specs=(P("pipe", "ep", None), P("pipe", "ep", None)),
        check_vma=False,
    )
```

```python
import jax
import jax.numpy as jnp
from jax import lax
from jax.sharding import PartitionSpec as P

EPS = 1e-06


def from_behind(block, axis, distance):
    devices = range(lax.axis_size(axis))
    route = [((i - distance) % len(devices), i) for i in devices]
    return lax.ppermute(block, axis, route)


def slot_places(ids, n_exp, cap):
    flat = ids.reshape(-1)
    onehot = (flat[:, None] == jnp.arange(n_exp, dtype=jnp.int32)[None, :]).astype(jnp.int32)
    before = jnp.cumsum(onehot, axis=0) - onehot
    slot = jnp.sum(before * onehot, axis=1)
    return flat * cap + slot


def rms_stats(x):
    xf = x.astype(jnp.float32)
    scale = lax.rsqrt(jnp.mean(xf * xf, axis=-1, keepdims=True) + EPS)
    return (xf, scale)


def expert_forward(rows, w_g, w_u, w_d):
    gate = jnp.dot(rows, w_g, preferred_element_type=jnp.float32)
    upper = jnp.dot(rows, w_u, preferred_element_type=jnp.float32)
    act = (jax.nn.silu(gate) * upper).astype(jnp.bfloat16)
    return jnp.dot(act, w_d, preferred_element_type=jnp.float32).astype(jnp.bfloat16)


def expert_backward(rows, cot, w_g, w_u, w_d):
    gate = jnp.dot(rows, w_g, preferred_element_type=jnp.float32)
    upper = jnp.dot(rows, w_u, preferred_element_type=jnp.float32)
    sigma = jax.nn.sigmoid(gate)
    dact = jnp.dot(cot, w_d.T, preferred_element_type=jnp.float32)
    dgate = (dact * upper * sigma * (1.0 + gate * (1.0 - sigma))).astype(jnp.bfloat16)
    dup = (dact * gate * sigma).astype(jnp.bfloat16)
    total = jnp.dot(dgate, w_g.T, preferred_element_type=jnp.float32) + jnp.dot(
        dup, w_u.T, preferred_element_type=jnp.float32
    )
    return total.astype(jnp.bfloat16)


def norm_backward(xf, scale, gain, upstream):
    scaled = gain * upstream
    inner = jnp.mean(xf * scaled, axis=-1, keepdims=True)
    return scale * scaled - xf * (scale * scale * scale) * inner


def expert_slots(ids_all, weights_all, me, cap):
    match = ids_all == me
    chosen = jnp.any(match, axis=-1)
    weight = jnp.sum(jnp.where(match, weights_all, 0.0), axis=-1)
    pos = jnp.cumsum(chosen.astype(jnp.int32), axis=1) - chosen.astype(jnp.int32)
    slot = jnp.arange(cap, dtype=jnp.int32)[None, :, None]
    onehot = chosen[:, None, :] & (pos[:, None, :] == slot)
    slot_w = jnp.sum(jnp.where(onehot, weight[:, None, :], 0.0), axis=-1)
    return onehot.astype(jnp.bfloat16), slot_w


def pick_rows(onehot, rows):
    picked = jnp.einsum("bct,btd->bcd", onehot, rows, preferred_element_type=jnp.float32)
    return picked.astype(jnp.bfloat16)


def combine_rows(places, back, top):
    count = back.shape[0]
    onehot = (places[:, None] == jnp.arange(count, dtype=jnp.int32)[None, :]).astype(jnp.bfloat16)
    picked = jnp.dot(onehot, back, preferred_element_type=jnp.float32)
    return picked.reshape(-1, top, back.shape[1])


def _pairs(n, n2, stage, move):
    out = []
    for i in range(n):
        e1, e2 = i // n2, i % n2
        if stage == 1:
            e1 = move(e1)
        else:
            e2 = move(e2)
        out.append((i, e1 * n2 + e2))
    return out


def gather_chain(parts, axis_name):
    n = lax.axis_size(axis_name)
    n2 = 4
    if n % n2 or any(v.shape[-1] % 128 for v in parts):
        return [lax.all_gather(v, axis_name, axis=0, tiled=False) for v in parts]
    n1 = n // n2
    me = lax.axis_index(axis_name)
    e1, e2 = me // n2, me % n2

    def along(part):
        s1 = jnp.zeros((n1,) + part.shape, part.dtype)
        s1 = lax.dynamic_update_index_in_dim(s1, part, e1, 0)
        for d in range(1, n1):
            got = lax.ppermute(part, axis_name, _pairs(n, n2, 1, lambda a: (a + d) % n1))
            s1 = lax.dynamic_update_index_in_dim(s1, got, (e1 - d) % n1, 0)
        return s1

    def across(s1):
        flip_x = lambda a: a ^ 1
        flip_y = lambda a: a ^ 2
        px = lax.ppermute(s1, axis_name, _pairs(n, n2, 2, flip_x))
        py = lax.ppermute(s1, axis_name, _pairs(n, n2, 2, flip_y))
        h = (s1.shape[-1] // 256) * 128
        d1 = lax.ppermute(px[..., :h], axis_name, _pairs(n, n2, 2, flip_y))
        d2 = lax.ppermute(py[..., h:], axis_name, _pairs(n, n2, 2, flip_x))
        diag = jnp.concatenate([d1, d2], axis=-1)
        s2 = jnp.zeros((n2,) + s1.shape, s1.dtype)
        s2 = lax.dynamic_update_index_in_dim(s2, s1, e2, 0)
        s2 = lax.dynamic_update_index_in_dim(s2, px, e2 ^ 1, 0)
        s2 = lax.dynamic_update_index_in_dim(s2, py, e2 ^ 2, 0)
        s2 = lax.dynamic_update_index_in_dim(s2, diag, e2 ^ 3, 0)
        return jnp.swapaxes(s2, 0, 1).reshape((n,) + s1.shape[1:])

    done = []
    ready = along(parts[0])
    for part in parts[1:]:
        ready, part = lax.optimization_barrier((ready, part))
        done.append(across(ready))
        ready = along(part)
        done[-1], ready = lax.optimization_barrier((done[-1], ready))
    done.append(across(ready))
    return done

def local(
    x_fwd, ids_fwd, route_fwd, x_bwd, grad_bwd, ids_bwd, route_bwd, norm_gain, w_gate, w_up, w_down
):
    n_exp = lax.axis_size("ep")
    me = lax.axis_index("ep")
    tok_dev = x_fwd.shape[1]
    width = x_fwd.shape[2]
    top = ids_fwd.shape[2]
    cap = 3 * tok_dev * top // (2 * n_exp)
    gain = norm_gain[0].astype(jnp.float32)
    w_g = w_gate[0, 0]
    w_u = w_up[0, 0]
    w_d = w_down[0, 0]
    xf, scale_f = rms_stats(x_fwd[0])
    h_f = (xf * scale_f * gain).astype(jnp.bfloat16)
    xb, scale_b = rms_stats(x_bwd[0])
    h_b = (xb * scale_b * gain).astype(jnp.bfloat16)
    grad = grad_bwd[0]
    weights_f = route_fwd[0] / jnp.sum(route_fwd[0], axis=-1, keepdims=True)
    weights_b = route_bwd[0] / jnp.sum(route_bwd[0], axis=-1, keepdims=True)

    def split3(r):
        hi = lax.reduce_precision(r, exponent_bits=8, mantissa_bits=7)
        rest = r - hi
        mid = lax.reduce_precision(rest, exponent_bits=8, mantissa_bits=7)
        return jnp.concatenate([hi, mid, rest - mid], axis=-1).astype(jnp.bfloat16)

    def join3(p):
        p = p.astype(jnp.float32)
        return (p[..., 0:top] + p[..., top:2 * top]) + p[..., 2 * top:3 * top]

    meta = jnp.concatenate(
        [ids_fwd[0].astype(jnp.bfloat16), ids_bwd[0].astype(jnp.bfloat16), split3(route_fwd[0]), split3(route_bwd[0])],
        axis=-1,
    )
    pad = (-meta.shape[-1]) % 128
    meta = jnp.concatenate([meta, jnp.zeros((tok_dev, pad), jnp.bfloat16)], axis=-1)
    message_f, all_h_b, all_g = gather_chain([jnp.concatenate([h_f, meta], axis=-1), h_b, grad], "ep")
    all_h_f = message_f[..., 0:width]
    got = message_f[..., width:]
    all_ids_f = got[..., 0:top].astype(jnp.int32)
    all_ids_b = got[..., top:2 * top].astype(jnp.int32)
    all_route_f = join3(got[..., 2 * top:5 * top])
    all_route_b = join3(got[..., 5 * top:8 * top])
    all_w_f = all_route_f / jnp.sum(all_route_f, axis=-1, keepdims=True)
    all_w_b = all_route_b / jnp.sum(all_route_b, axis=-1, keepdims=True)

    onehot_f, _ = expert_slots(all_ids_f, all_w_f, me, cap)
    rows = pick_rows(onehot_f, all_h_f).reshape(-1, width)
    made_f = expert_forward(rows, w_g, w_u, w_d).reshape(n_exp, cap, width)
    back_f = lax.all_to_all(made_f, "ep", split_axis=0, concat_axis=0, tiled=True)

    onehot_b, slot_w_b = expert_slots(all_ids_b, all_w_b, me, cap)
    rows = pick_rows(onehot_b, all_h_b).reshape(-1, width)
    g_rows = pick_rows(onehot_b, all_g)
    cots = (slot_w_b[:, :, None] * g_rows.astype(jnp.float32)).astype(jnp.bfloat16).reshape(-1, width)
    made_b = expert_backward(rows, cots, w_g, w_u, w_d).reshape(n_exp, cap, width)
    back_b = lax.all_to_all(made_b, "ep", split_axis=0, concat_axis=0, tiled=True)

    places_f = slot_places(ids_fwd[0], n_exp, cap)
    picked_f = combine_rows(places_f, back_f.reshape(-1, width), top)
    mixed = jnp.sum(weights_f[:, :, None] * picked_f, axis=1)
    layer_out = (xf + mixed).astype(jnp.bfloat16)[None]
    places_b = slot_places(ids_bwd[0], n_exp, cap)
    picked_b = combine_rows(places_b, back_b.reshape(-1, width), top)
    dnorm = jnp.sum(picked_b, axis=1)
    input_grad = (grad.astype(jnp.float32) + norm_backward(xb, scale_b, gain, dnorm)).astype(
        jnp.bfloat16
    )[None]
    fwd_next = from_behind(layer_out, "pipe", 1)
    bwd_prev = from_behind(input_grad, "pipe", -1)
    return (fwd_next, bwd_prev)


def solution(mesh):
    placed = (
        P("pipe", "ep", None),
        P("pipe", "ep", None),
        P("pipe", "ep", None),
        P("pipe", "ep", None),
        P("pipe", "ep", None),
        P("pipe", "ep", None),
        P("pipe", "ep", None),
        P("pipe", None),
        P("pipe", "ep", None, None),
        P("pipe", "ep", None, None),
        P("pipe", "ep", None, None),
    )
    return jax.shard_map(
        local,
        mesh=mesh,
        in_specs=placed,
        out_specs=(P("pipe", "ep", None), P("pipe", "ep", None)),
        check_vma=False,
    )
```

```python
import jax
import jax.numpy as jnp
from jax import lax
from jax.sharding import PartitionSpec as P

EPS = 1e-06


def from_behind(block, axis, distance):
    devices = range(lax.axis_size(axis))
    route = [((i - distance) % len(devices), i) for i in devices]
    return lax.ppermute(block, axis, route)


def slot_places(ids, n_exp, cap):
    flat = ids.reshape(-1)
    onehot = (flat[:, None] == jnp.arange(n_exp, dtype=jnp.int32)[None, :]).astype(jnp.int32)
    before = jnp.cumsum(onehot, axis=0) - onehot
    slot = jnp.sum(before * onehot, axis=1)
    return flat * cap + slot


def rms_stats(x):
    xf = x.astype(jnp.float32)
    scale = lax.rsqrt(jnp.mean(xf * xf, axis=-1, keepdims=True) + EPS)
    return (xf, scale)


def expert_forward(rows, w_g, w_u, w_d):
    gate = jnp.dot(rows, w_g, preferred_element_type=jnp.float32)
    upper = jnp.dot(rows, w_u, preferred_element_type=jnp.float32)
    act = (jax.nn.silu(gate) * upper).astype(jnp.bfloat16)
    return jnp.dot(act, w_d, preferred_element_type=jnp.float32).astype(jnp.bfloat16)


def expert_backward(rows, cot, w_g, w_u, w_d):
    gate = jnp.dot(rows, w_g, preferred_element_type=jnp.float32)
    upper = jnp.dot(rows, w_u, preferred_element_type=jnp.float32)
    sigma = jax.nn.sigmoid(gate)
    dact = jnp.dot(cot, w_d.T, preferred_element_type=jnp.float32)
    dgate = (dact * upper * sigma * (1.0 + gate * (1.0 - sigma))).astype(jnp.bfloat16)
    dup = (dact * gate * sigma).astype(jnp.bfloat16)
    total = jnp.dot(dgate, w_g.T, preferred_element_type=jnp.float32) + jnp.dot(
        dup, w_u.T, preferred_element_type=jnp.float32
    )
    return total.astype(jnp.bfloat16)


def expert_backward_parts(rows, cot, w_g, w_u, w_d, parts):
    gate = jnp.dot(rows, w_g, preferred_element_type=jnp.float32)
    upper = jnp.dot(rows, w_u, preferred_element_type=jnp.float32)
    sigma = jax.nn.sigmoid(gate)
    dact = jnp.dot(cot, w_d.T, preferred_element_type=jnp.float32)
    dgate = (dact * upper * sigma * (1.0 + gate * (1.0 - sigma))).astype(jnp.bfloat16)
    dup = (dact * gate * sigma).astype(jnp.bfloat16)
    step = w_g.shape[0] // parts
    out = []
    for p in range(parts):
        cols = slice(p * step, (p + 1) * step)
        total = jnp.dot(dgate, w_g[cols].T, preferred_element_type=jnp.float32) + jnp.dot(
            dup, w_u[cols].T, preferred_element_type=jnp.float32
        )
        out.append(total.astype(jnp.bfloat16))
    return out


def norm_backward(xf, scale, gain, upstream):
    scaled = gain * upstream
    inner = jnp.mean(xf * scaled, axis=-1, keepdims=True)
    return scale * scaled - xf * (scale * scale * scale) * inner


def expert_slots(ids_all, weights_all, me, cap):
    match = ids_all == me
    chosen = jnp.any(match, axis=-1)
    weight = jnp.sum(jnp.where(match, weights_all, 0.0), axis=-1)
    pos = jnp.cumsum(chosen.astype(jnp.int32), axis=1) - chosen.astype(jnp.int32)
    slot = jnp.arange(cap, dtype=jnp.int32)[None, :, None]
    onehot = chosen[:, None, :] & (pos[:, None, :] == slot)
    slot_w = jnp.sum(jnp.where(onehot, weight[:, None, :], 0.0), axis=-1)
    return onehot.astype(jnp.bfloat16), slot_w


def pick_rows(onehot, rows):
    picked = jnp.einsum("bct,btd->bcd", onehot, rows, preferred_element_type=jnp.float32)
    return picked.astype(jnp.bfloat16)


def combine_rows(places, back, top):
    count = back.shape[0]
    onehot = (places[:, None] == jnp.arange(count, dtype=jnp.int32)[None, :]).astype(jnp.bfloat16)
    picked = jnp.dot(onehot, back, preferred_element_type=jnp.float32)
    return picked.reshape(-1, top, back.shape[1])


def _pairs(n, n2, stage, move):
    out = []
    for i in range(n):
        e1, e2 = i // n2, i % n2
        if stage == 1:
            e1 = move(e1)
        else:
            e2 = move(e2)
        out.append((i, e1 * n2 + e2))
    return out


def gather_chain(parts, axis_name):
    n = lax.axis_size(axis_name)
    n2 = 4
    if n % n2 or any(v.shape[-1] % 128 for v in parts):
        return [lax.all_gather(v, axis_name, axis=0, tiled=False) for v in parts]
    n1 = n // n2
    me = lax.axis_index(axis_name)
    e1, e2 = me // n2, me % n2

    def along(part):
        s1 = jnp.zeros((n1,) + part.shape, part.dtype)
        s1 = lax.dynamic_update_index_in_dim(s1, part, e1, 0)
        for d in range(1, n1):
            got = lax.ppermute(part, axis_name, _pairs(n, n2, 1, lambda a: (a + d) % n1))
            s1 = lax.dynamic_update_index_in_dim(s1, got, (e1 - d) % n1, 0)
        return s1

    def across(s1):
        flip_x = lambda a: a ^ 1
        flip_y = lambda a: a ^ 2
        px = lax.ppermute(s1, axis_name, _pairs(n, n2, 2, flip_x))
        py = lax.ppermute(s1, axis_name, _pairs(n, n2, 2, flip_y))
        h = (s1.shape[-1] // 256) * 128
        d1 = lax.ppermute(px[..., :h], axis_name, _pairs(n, n2, 2, flip_y))
        d2 = lax.ppermute(py[..., h:], axis_name, _pairs(n, n2, 2, flip_x))
        diag = jnp.concatenate([d1, d2], axis=-1)
        s2 = jnp.zeros((n2,) + s1.shape, s1.dtype)
        s2 = lax.dynamic_update_index_in_dim(s2, s1, e2, 0)
        s2 = lax.dynamic_update_index_in_dim(s2, px, e2 ^ 1, 0)
        s2 = lax.dynamic_update_index_in_dim(s2, py, e2 ^ 2, 0)
        s2 = lax.dynamic_update_index_in_dim(s2, diag, e2 ^ 3, 0)
        return jnp.swapaxes(s2, 0, 1).reshape((n,) + s1.shape[1:])

    done = []
    ready = along(parts[0])
    for part in parts[1:]:
        ready, part = lax.optimization_barrier((ready, part))
        done.append(across(ready))
        ready = along(part)
        done[-1], ready = lax.optimization_barrier((done[-1], ready))
    done.append(across(ready))
    return done

def local(
    x_fwd, ids_fwd, route_fwd, x_bwd, grad_bwd, ids_bwd, route_bwd, norm_gain, w_gate, w_up, w_down
):
    n_exp = lax.axis_size("ep")
    me = lax.axis_index("ep")
    tok_dev = x_fwd.shape[1]
    width = x_fwd.shape[2]
    top = ids_fwd.shape[2]
    cap = 3 * tok_dev * top // (2 * n_exp)
    gain = norm_gain[0].astype(jnp.float32)
    w_g = w_gate[0, 0]
    w_u = w_up[0, 0]
    w_d = w_down[0, 0]
    xf, scale_f = rms_stats(x_fwd[0])
    h_f = (xf * scale_f * gain).astype(jnp.bfloat16)
    xb, scale_b = rms_stats(x_bwd[0])
    h_b = (xb * scale_b * gain).astype(jnp.bfloat16)
    grad = grad_bwd[0]
    weights_f = route_fwd[0] / jnp.sum(route_fwd[0], axis=-1, keepdims=True)
    weights_b = route_bwd[0] / jnp.sum(route_bwd[0], axis=-1, keepdims=True)

    def split3(r):
        hi = lax.reduce_precision(r, exponent_bits=8, mantissa_bits=7)
        rest = r - hi
        mid = lax.reduce_precision(rest, exponent_bits=8, mantissa_bits=7)
        return jnp.concatenate([hi, mid, rest - mid], axis=-1).astype(jnp.bfloat16)

    def join3(p):
        p = p.astype(jnp.float32)
        return (p[..., 0:top] + p[..., top:2 * top]) + p[..., 2 * top:3 * top]

    meta = jnp.concatenate(
        [ids_fwd[0].astype(jnp.bfloat16), ids_bwd[0].astype(jnp.bfloat16), split3(route_fwd[0]), split3(route_bwd[0])],
        axis=-1,
    )
    pad = (-meta.shape[-1]) % 128
    meta = jnp.concatenate([meta, jnp.zeros((tok_dev, pad), jnp.bfloat16)], axis=-1)
    message_f, all_h_b, all_g = gather_chain([jnp.concatenate([h_f, meta], axis=-1), h_b, grad], "ep")
    all_h_f = message_f[..., 0:width]
    got = message_f[..., width:]
    all_ids_f = got[..., 0:top].astype(jnp.int32)
    all_ids_b = got[..., top:2 * top].astype(jnp.int32)
    all_route_f = join3(got[..., 2 * top:5 * top])
    all_route_b = join3(got[..., 5 * top:8 * top])
    all_w_f = all_route_f / jnp.sum(all_route_f, axis=-1, keepdims=True)
    all_w_b = all_route_b / jnp.sum(all_route_b, axis=-1, keepdims=True)

    onehot_f, _ = expert_slots(all_ids_f, all_w_f, me, cap)
    rows = pick_rows(onehot_f, all_h_f).reshape(-1, width)
    made_f = expert_forward(rows, w_g, w_u, w_d).reshape(n_exp, cap, width)
    back_f = lax.all_to_all(made_f, "ep", split_axis=0, concat_axis=0, tiled=True)

    onehot_b, slot_w_b = expert_slots(all_ids_b, all_w_b, me, cap)
    rows = pick_rows(onehot_b, all_h_b).reshape(-1, width)
    g_rows = pick_rows(onehot_b, all_g)
    cots = (slot_w_b[:, :, None] * g_rows.astype(jnp.float32)).astype(jnp.bfloat16).reshape(-1, width)
    parts = 2 if width % 256 == 0 else 1
    back_b = [
        lax.all_to_all(made.reshape(n_exp, cap, -1), "ep", split_axis=0, concat_axis=0, tiled=True)
        for made in expert_backward_parts(rows, cots, w_g, w_u, w_d, parts)
    ]

    places_f = slot_places(ids_fwd[0], n_exp, cap)
    picked_f = combine_rows(places_f, back_f.reshape(-1, width), top)
    mixed = jnp.sum(weights_f[:, :, None] * picked_f, axis=1)
    layer_out = (xf + mixed).astype(jnp.bfloat16)[None]
    places_b = slot_places(ids_bwd[0], n_exp, cap)
    dnorm = jnp.concatenate(
        [jnp.sum(combine_rows(places_b, part.reshape(n_exp * cap, -1), top), axis=1) for part in back_b], axis=-1
    )
    input_grad = (grad.astype(jnp.float32) + norm_backward(xb, scale_b, gain, dnorm)).astype(
        jnp.bfloat16
    )[None]
    fwd_next = from_behind(layer_out, "pipe", 1)
    bwd_prev = from_behind(input_grad, "pipe", -1)
    return (fwd_next, bwd_prev)


def solution(mesh):
    placed = (
        P("pipe", "ep", None),
        P("pipe", "ep", None),
        P("pipe", "ep", None),
        P("pipe", "ep", None),
        P("pipe", "ep", None),
        P("pipe", "ep", None),
        P("pipe", "ep", None),
        P("pipe", None),
        P("pipe", "ep", None, None),
        P("pipe", "ep", None, None),
        P("pipe", "ep", None, None),
    )
    return jax.shard_map(
        local,
        mesh=mesh,
        in_specs=placed,
        out_specs=(P("pipe", "ep", None), P("pipe", "ep", None)),
        check_vma=False,
    )
```

```python
import jax
import jax.numpy as jnp
from jax import lax
from jax.sharding import PartitionSpec as P

EPS = 1e-06


def from_behind(block, axis, distance):
    devices = range(lax.axis_size(axis))
    route = [((i - distance) % len(devices), i) for i in devices]
    return lax.ppermute(block, axis, route)


def slot_places(ids, n_exp, cap):
    flat = ids.reshape(-1)
    onehot = (flat[:, None] == jnp.arange(n_exp, dtype=jnp.int32)[None, :]).astype(jnp.int32)
    before = jnp.cumsum(onehot, axis=0) - onehot
    slot = jnp.sum(before * onehot, axis=1)
    return flat * cap + slot


def rms_stats(x):
    xf = x.astype(jnp.float32)
    scale = lax.rsqrt(jnp.mean(xf * xf, axis=-1, keepdims=True) + EPS)
    return (xf, scale)


def expert_forward(rows, w_g, w_u, w_d):
    gate = jnp.dot(rows, w_g, preferred_element_type=jnp.float32)
    upper = jnp.dot(rows, w_u, preferred_element_type=jnp.float32)
    act = (jax.nn.silu(gate) * upper).astype(jnp.bfloat16)
    return jnp.dot(act, w_d, preferred_element_type=jnp.float32).astype(jnp.bfloat16)


def expert_backward(rows, cot, w_g, w_u, w_d):
    gate = jnp.dot(rows, w_g, preferred_element_type=jnp.float32)
    upper = jnp.dot(rows, w_u, preferred_element_type=jnp.float32)
    sigma = jax.nn.sigmoid(gate)
    dact = jnp.dot(cot, w_d.T, preferred_element_type=jnp.float32)
    dgate = (dact * upper * sigma * (1.0 + gate * (1.0 - sigma))).astype(jnp.bfloat16)
    dup = (dact * gate * sigma).astype(jnp.bfloat16)
    total = jnp.dot(dgate, w_g.T, preferred_element_type=jnp.float32) + jnp.dot(
        dup, w_u.T, preferred_element_type=jnp.float32
    )
    return total.astype(jnp.bfloat16)


def expert_backward_parts(rows, cot, w_g, w_u, w_d, parts):
    gate = jnp.dot(rows, w_g, preferred_element_type=jnp.float32)
    upper = jnp.dot(rows, w_u, preferred_element_type=jnp.float32)
    sigma = jax.nn.sigmoid(gate)
    dact = jnp.dot(cot, w_d.T, preferred_element_type=jnp.float32)
    dgate = (dact * upper * sigma * (1.0 + gate * (1.0 - sigma))).astype(jnp.bfloat16)
    dup = (dact * gate * sigma).astype(jnp.bfloat16)
    step = w_g.shape[0] // parts
    out = []
    for p in range(parts):
        cols = slice(p * step, (p + 1) * step)
        total = jnp.dot(dgate, w_g[cols].T, preferred_element_type=jnp.float32) + jnp.dot(
            dup, w_u[cols].T, preferred_element_type=jnp.float32
        )
        out.append(total.astype(jnp.bfloat16))
    return out


def norm_backward(xf, scale, gain, upstream):
    scaled = gain * upstream
    inner = jnp.mean(xf * scaled, axis=-1, keepdims=True)
    return scale * scaled - xf * (scale * scale * scale) * inner


def expert_slots(ids_all, weights_all, me, cap):
    match = ids_all == me
    chosen = jnp.any(match, axis=-1)
    weight = jnp.sum(jnp.where(match, weights_all, 0.0), axis=-1)
    pos = jnp.cumsum(chosen.astype(jnp.int32), axis=1) - chosen.astype(jnp.int32)
    slot = jnp.arange(cap, dtype=jnp.int32)[None, :, None]
    onehot = chosen[:, None, :] & (pos[:, None, :] == slot)
    slot_w = jnp.sum(jnp.where(onehot, weight[:, None, :], 0.0), axis=-1)
    return onehot.astype(jnp.bfloat16), slot_w


def pick_rows(onehot, rows):
    picked = jnp.einsum("bct,btd->bcd", onehot, rows, preferred_element_type=jnp.float32)
    return picked.astype(jnp.bfloat16)


def combine_rows(places, back, top):
    count = back.shape[0]
    onehot = (places[:, None] == jnp.arange(count, dtype=jnp.int32)[None, :]).astype(jnp.bfloat16)
    picked = jnp.dot(onehot, back, preferred_element_type=jnp.float32)
    return picked.reshape(-1, top, back.shape[1])


def _pairs(n, n2, stage, move):
    out = []
    for i in range(n):
        e1, e2 = i // n2, i % n2
        if stage == 1:
            e1 = move(e1)
        else:
            e2 = move(e2)
        out.append((i, e1 * n2 + e2))
    return out


def gather_chain(parts, axis_name):
    n = lax.axis_size(axis_name)
    n2 = 4
    if n % n2 or any(v.shape[-1] % 128 for v in parts):
        return [lax.all_gather(v, axis_name, axis=0, tiled=False) for v in parts]
    n1 = n // n2
    me = lax.axis_index(axis_name)
    e1, e2 = me // n2, me % n2

    def along(part):
        s1 = jnp.zeros((n1,) + part.shape, part.dtype)
        s1 = lax.dynamic_update_index_in_dim(s1, part, e1, 0)
        for d in range(1, n1):
            got = lax.ppermute(part, axis_name, _pairs(n, n2, 1, lambda a: (a + d) % n1))
            s1 = lax.dynamic_update_index_in_dim(s1, got, (e1 - d) % n1, 0)
        return s1

    def across(s1):
        flip_x = lambda a: a ^ 1
        flip_y = lambda a: a ^ 2
        px = lax.ppermute(s1, axis_name, _pairs(n, n2, 2, flip_x))
        py = lax.ppermute(s1, axis_name, _pairs(n, n2, 2, flip_y))
        h = (s1.shape[-1] // 256) * 128
        d1 = lax.ppermute(px[..., :h], axis_name, _pairs(n, n2, 2, flip_y))
        d2 = lax.ppermute(py[..., h:], axis_name, _pairs(n, n2, 2, flip_x))
        diag = jnp.concatenate([d1, d2], axis=-1)
        s2 = jnp.zeros((n2,) + s1.shape, s1.dtype)
        s2 = lax.dynamic_update_index_in_dim(s2, s1, e2, 0)
        s2 = lax.dynamic_update_index_in_dim(s2, px, e2 ^ 1, 0)
        s2 = lax.dynamic_update_index_in_dim(s2, py, e2 ^ 2, 0)
        s2 = lax.dynamic_update_index_in_dim(s2, diag, e2 ^ 3, 0)
        return jnp.swapaxes(s2, 0, 1).reshape((n,) + s1.shape[1:])

    done = []
    ready = along(parts[0])
    for part in parts[1:]:
        ready, part = lax.optimization_barrier((ready, part))
        done.append(across(ready))
        ready = along(part)
        done[-1], ready = lax.optimization_barrier((done[-1], ready))
    done.append(across(ready))
    return done

def local(
    x_fwd, ids_fwd, route_fwd, x_bwd, grad_bwd, ids_bwd, route_bwd, norm_gain, w_gate, w_up, w_down
):
    n_exp = lax.axis_size("ep")
    me = lax.axis_index("ep")
    tok_dev = x_fwd.shape[1]
    width = x_fwd.shape[2]
    top = ids_fwd.shape[2]
    cap = 3 * tok_dev * top // (2 * n_exp)
    gain = norm_gain[0].astype(jnp.float32)
    w_g = w_gate[0, 0]
    w_u = w_up[0, 0]
    w_d = w_down[0, 0]
    xf, scale_f = rms_stats(x_fwd[0])
    h_f = (xf * scale_f * gain).astype(jnp.bfloat16)
    xb, scale_b = rms_stats(x_bwd[0])
    h_b = (xb * scale_b * gain).astype(jnp.bfloat16)
    grad = grad_bwd[0]
    weights_f = route_fwd[0] / jnp.sum(route_fwd[0], axis=-1, keepdims=True)
    weights_b = route_bwd[0] / jnp.sum(route_bwd[0], axis=-1, keepdims=True)

    def split3(r):
        hi = lax.reduce_precision(r, exponent_bits=8, mantissa_bits=7)
        rest = r - hi
        mid = lax.reduce_precision(rest, exponent_bits=8, mantissa_bits=7)
        return jnp.concatenate([hi, mid, rest - mid], axis=-1).astype(jnp.bfloat16)

    def join3(p):
        p = p.astype(jnp.float32)
        k = p.shape[-1] // 3
        return (p[..., 0:k] + p[..., k:2 * k]) + p[..., 2 * k:3 * k]

    table = jnp.concatenate(
        [ids_fwd[0].astype(jnp.float32), ids_bwd[0].astype(jnp.float32), route_fwd[0], route_bwd[0]], axis=-1
    )
    meta = split3(table)
    pad = (-meta.shape[-1]) % 128
    meta = jnp.concatenate([meta, jnp.zeros((tok_dev, pad), jnp.bfloat16)], axis=-1)
    message_f, all_h_b, all_g = gather_chain([jnp.concatenate([h_f, meta], axis=-1), h_b, grad], "ep")
    all_h_f = message_f[..., 0:width]
    got = join3(message_f[..., width:width + 3 * table.shape[-1]])
    all_ids_f = got[..., 0:top].astype(jnp.int32)
    all_ids_b = got[..., top:2 * top].astype(jnp.int32)
    all_route_f = got[..., 2 * top:3 * top]
    all_route_b = got[..., 3 * top:4 * top]
    all_w_f = all_route_f / jnp.sum(all_route_f, axis=-1, keepdims=True)
    all_w_b = all_route_b / jnp.sum(all_route_b, axis=-1, keepdims=True)

    onehot_f, _ = expert_slots(all_ids_f, all_w_f, me, cap)
    rows = pick_rows(onehot_f, all_h_f).reshape(-1, width)
    made_f = expert_forward(rows, w_g, w_u, w_d).reshape(n_exp, cap, width)
    back_f = lax.all_to_all(made_f, "ep", split_axis=0, concat_axis=0, tiled=True)

    onehot_b, slot_w_b = expert_slots(all_ids_b, all_w_b, me, cap)
    rows = pick_rows(onehot_b, all_h_b).reshape(-1, width)
    g_rows = pick_rows(onehot_b, all_g)
    cots = (slot_w_b[:, :, None] * g_rows.astype(jnp.float32)).astype(jnp.bfloat16).reshape(-1, width)
    parts = 2 if width % 256 == 0 else 1
    back_b = [
        lax.all_to_all(made.reshape(n_exp, cap, -1), "ep", split_axis=0, concat_axis=0, tiled=True)
        for made in expert_backward_parts(rows, cots, w_g, w_u, w_d, parts)
    ]

    places_f = slot_places(ids_fwd[0], n_exp, cap)
    picked_f = combine_rows(places_f, back_f.reshape(-1, width), top)
    mixed = jnp.sum(weights_f[:, :, None] * picked_f, axis=1)
    layer_out = (xf + mixed).astype(jnp.bfloat16)[None]
    places_b = slot_places(ids_bwd[0], n_exp, cap)
    dnorm = jnp.concatenate(
        [jnp.sum(combine_rows(places_b, part.reshape(n_exp * cap, -1), top), axis=1) for part in back_b], axis=-1
    )
    input_grad = (grad.astype(jnp.float32) + norm_backward(xb, scale_b, gain, dnorm)).astype(
        jnp.bfloat16
    )[None]
    fwd_next = from_behind(layer_out, "pipe", 1)
    bwd_prev = from_behind(input_grad, "pipe", -1)
    return (fwd_next, bwd_prev)


def solution(mesh):
    placed = (
        P("pipe", "ep", None),
        P("pipe", "ep", None),
        P("pipe", "ep", None),
        P("pipe", "ep", None),
        P("pipe", "ep", None),
        P("pipe", "ep", None),
        P("pipe", "ep", None),
        P("pipe", None),
        P("pipe", "ep", None, None),
        P("pipe", "ep", None, None),
        P("pipe", "ep", None, None),
    )
    return jax.shard_map(
        local,
        mesh=mesh,
        in_specs=placed,
        out_specs=(P("pipe", "ep", None), P("pipe", "ep", None)),
        check_vma=False,
    )
```

```python
import jax
import jax.numpy as jnp
from jax import lax
from jax.sharding import PartitionSpec as P

EPS = 1e-06


def from_behind(block, axis, distance):
    devices = range(lax.axis_size(axis))
    route = [((i - distance) % len(devices), i) for i in devices]
    return lax.ppermute(block, axis, route)


def slot_places(ids, n_exp, cap):
    flat = ids.reshape(-1)
    onehot = (flat[:, None] == jnp.arange(n_exp, dtype=jnp.int32)[None, :]).astype(jnp.int32)
    before = jnp.cumsum(onehot, axis=0) - onehot
    slot = jnp.sum(before * onehot, axis=1)
    return flat * cap + slot


def rms_stats(x):
    xf = x.astype(jnp.float32)
    scale = lax.rsqrt(jnp.mean(xf * xf, axis=-1, keepdims=True) + EPS)
    return (xf, scale)


def expert_forward(rows, w_g, w_u, w_d):
    gate = jnp.dot(rows, w_g, preferred_element_type=jnp.float32)
    upper = jnp.dot(rows, w_u, preferred_element_type=jnp.float32)
    act = (jax.nn.silu(gate) * upper).astype(jnp.bfloat16)
    return jnp.dot(act, w_d, preferred_element_type=jnp.float32).astype(jnp.bfloat16)


def expert_backward(rows, cot, w_g, w_u, w_d):
    gate = jnp.dot(rows, w_g, preferred_element_type=jnp.float32)
    upper = jnp.dot(rows, w_u, preferred_element_type=jnp.float32)
    sigma = jax.nn.sigmoid(gate)
    dact = jnp.dot(cot, w_d.T, preferred_element_type=jnp.float32)
    dgate = (dact * upper * sigma * (1.0 + gate * (1.0 - sigma))).astype(jnp.bfloat16)
    dup = (dact * gate * sigma).astype(jnp.bfloat16)
    total = jnp.dot(dgate, w_g.T, preferred_element_type=jnp.float32) + jnp.dot(
        dup, w_u.T, preferred_element_type=jnp.float32
    )
    return total.astype(jnp.bfloat16)


def expert_backward_parts(rows, cot, w_g, w_u, w_d, parts):
    gate = jnp.dot(rows, w_g, preferred_element_type=jnp.float32)
    upper = jnp.dot(rows, w_u, preferred_element_type=jnp.float32)
    sigma = jax.nn.sigmoid(gate)
    dact = jnp.dot(cot, w_d.T, preferred_element_type=jnp.float32)
    dgate = (dact * upper * sigma * (1.0 + gate * (1.0 - sigma))).astype(jnp.bfloat16)
    dup = (dact * gate * sigma).astype(jnp.bfloat16)
    cut = (3 * w_g.shape[0] // 4) // 128 * 128 if parts == 2 else w_g.shape[0]
    bounds = [0, cut, w_g.shape[0]][: parts + 1]
    out = []
    for p in range(parts):
        cols = slice(bounds[p], bounds[p + 1])
        total = jnp.dot(dgate, w_g[cols].T, preferred_element_type=jnp.float32) + jnp.dot(
            dup, w_u[cols].T, preferred_element_type=jnp.float32
        )
        out.append(total.astype(jnp.bfloat16))
    return out


def norm_backward(xf, scale, gain, upstream):
    scaled = gain * upstream
    inner = jnp.mean(xf * scaled, axis=-1, keepdims=True)
    return scale * scaled - xf * (scale * scale * scale) * inner


def expert_slots(ids_all, weights_all, me, cap):
    match = ids_all == me
    chosen = jnp.any(match, axis=-1)
    weight = jnp.sum(jnp.where(match, weights_all, 0.0), axis=-1)
    pos = jnp.cumsum(chosen.astype(jnp.int32), axis=1) - chosen.astype(jnp.int32)
    slot = jnp.arange(cap, dtype=jnp.int32)[None, :, None]
    onehot = chosen[:, None, :] & (pos[:, None, :] == slot)
    slot_w = jnp.sum(jnp.where(onehot, weight[:, None, :], 0.0), axis=-1)
    return onehot.astype(jnp.bfloat16), slot_w


def pick_rows(onehot, rows):
    picked = jnp.einsum("bct,btd->bcd", onehot, rows, preferred_element_type=jnp.float32)
    return picked.astype(jnp.bfloat16)


def combine_rows(places, back, top):
    count = back.shape[0]
    onehot = (places[:, None] == jnp.arange(count, dtype=jnp.int32)[None, :]).astype(jnp.bfloat16)
    picked = jnp.dot(onehot, back, preferred_element_type=jnp.float32)
    return picked.reshape(-1, top, back.shape[1])


def _pairs(n, n2, stage, move):
    out = []
    for i in range(n):
        e1, e2 = i // n2, i % n2
        if stage == 1:
            e1 = move(e1)
        else:
            e2 = move(e2)
        out.append((i, e1 * n2 + e2))
    return out


def gather_chain(parts, axis_name):
    n = lax.axis_size(axis_name)
    n2 = 4
    if n % n2 or any(v.shape[-1] % 128 for v in parts):
        return [lax.all_gather(v, axis_name, axis=0, tiled=False) for v in parts]
    n1 = n // n2
    me = lax.axis_index(axis_name)
    e1, e2 = me // n2, me % n2

    def along(part):
        s1 = jnp.zeros((n1,) + part.shape, part.dtype)
        s1 = lax.dynamic_update_index_in_dim(s1, part, e1, 0)
        for d in range(1, n1):
            got = lax.ppermute(part, axis_name, _pairs(n, n2, 1, lambda a: (a + d) % n1))
            s1 = lax.dynamic_update_index_in_dim(s1, got, (e1 - d) % n1, 0)
        return s1

    def across(s1):
        flip_x = lambda a: a ^ 1
        flip_y = lambda a: a ^ 2
        px = lax.ppermute(s1, axis_name, _pairs(n, n2, 2, flip_x))
        py = lax.ppermute(s1, axis_name, _pairs(n, n2, 2, flip_y))
        h = (s1.shape[-1] // 256) * 128
        d1 = lax.ppermute(px[..., :h], axis_name, _pairs(n, n2, 2, flip_y))
        d2 = lax.ppermute(py[..., h:], axis_name, _pairs(n, n2, 2, flip_x))
        diag = jnp.concatenate([d1, d2], axis=-1)
        s2 = jnp.zeros((n2,) + s1.shape, s1.dtype)
        s2 = lax.dynamic_update_index_in_dim(s2, s1, e2, 0)
        s2 = lax.dynamic_update_index_in_dim(s2, px, e2 ^ 1, 0)
        s2 = lax.dynamic_update_index_in_dim(s2, py, e2 ^ 2, 0)
        s2 = lax.dynamic_update_index_in_dim(s2, diag, e2 ^ 3, 0)
        return jnp.swapaxes(s2, 0, 1).reshape((n,) + s1.shape[1:])

    done = []
    ready = along(parts[0])
    for part in parts[1:]:
        ready, part = lax.optimization_barrier((ready, part))
        done.append(across(ready))
        ready = along(part)
        done[-1], ready = lax.optimization_barrier((done[-1], ready))
    done.append(across(ready))
    return done

def local(
    x_fwd, ids_fwd, route_fwd, x_bwd, grad_bwd, ids_bwd, route_bwd, norm_gain, w_gate, w_up, w_down
):
    n_exp = lax.axis_size("ep")
    me = lax.axis_index("ep")
    tok_dev = x_fwd.shape[1]
    width = x_fwd.shape[2]
    top = ids_fwd.shape[2]
    cap = 3 * tok_dev * top // (2 * n_exp)
    gain = norm_gain[0].astype(jnp.float32)
    w_g = w_gate[0, 0]
    w_u = w_up[0, 0]
    w_d = w_down[0, 0]
    xf, scale_f = rms_stats(x_fwd[0])
    h_f = (xf * scale_f * gain).astype(jnp.bfloat16)
    xb, scale_b = rms_stats(x_bwd[0])
    h_b = (xb * scale_b * gain).astype(jnp.bfloat16)
    grad = grad_bwd[0]
    weights_f = route_fwd[0] / jnp.sum(route_fwd[0], axis=-1, keepdims=True)
    weights_b = route_bwd[0] / jnp.sum(route_bwd[0], axis=-1, keepdims=True)

    def split3(r):
        hi = lax.reduce_precision(r, exponent_bits=8, mantissa_bits=7)
        rest = r - hi
        mid = lax.reduce_precision(rest, exponent_bits=8, mantissa_bits=7)
        return jnp.concatenate([hi, mid, rest - mid], axis=-1).astype(jnp.bfloat16)

    def join3(p):
        p = p.astype(jnp.float32)
        k = p.shape[-1] // 3
        return (p[..., 0:k] + p[..., k:2 * k]) + p[..., 2 * k:3 * k]

    table = jnp.concatenate(
        [ids_fwd[0].astype(jnp.float32), ids_bwd[0].astype(jnp.float32), route_fwd[0], route_bwd[0]], axis=-1
    )
    meta = split3(table)
    pad = (-meta.shape[-1]) % 128
    meta = jnp.concatenate([meta, jnp.zeros((tok_dev, pad), jnp.bfloat16)], axis=-1)
    message_f, all_h_b, all_g = gather_chain([jnp.concatenate([h_f, meta], axis=-1), h_b, grad], "ep")
    all_h_f = message_f[..., 0:width]
    got = join3(message_f[..., width:width + 3 * table.shape[-1]])
    all_ids_f = got[..., 0:top].astype(jnp.int32)
    all_ids_b = got[..., top:2 * top].astype(jnp.int32)
    all_route_f = got[..., 2 * top:3 * top]
    all_route_b = got[..., 3 * top:4 * top]
    all_w_f = all_route_f / jnp.sum(all_route_f, axis=-1, keepdims=True)
    all_w_b = all_route_b / jnp.sum(all_route_b, axis=-1, keepdims=True)

    onehot_f, _ = expert_slots(all_ids_f, all_w_f, me, cap)
    rows = pick_rows(onehot_f, all_h_f).reshape(-1, width)
    made_f = expert_forward(rows, w_g, w_u, w_d).reshape(n_exp, cap, width)
    back_f = lax.all_to_all(made_f, "ep", split_axis=0, concat_axis=0, tiled=True)

    onehot_b, slot_w_b = expert_slots(all_ids_b, all_w_b, me, cap)
    rows = pick_rows(onehot_b, all_h_b).reshape(-1, width)
    g_rows = pick_rows(onehot_b, all_g)
    cots = (slot_w_b[:, :, None] * g_rows.astype(jnp.float32)).astype(jnp.bfloat16).reshape(-1, width)
    parts = 2 if width % 256 == 0 else 1
    back_b = [
        lax.all_to_all(made.reshape(n_exp, cap, -1), "ep", split_axis=0, concat_axis=0, tiled=True)
        for made in expert_backward_parts(rows, cots, w_g, w_u, w_d, parts)
    ]

    places_f = slot_places(ids_fwd[0], n_exp, cap)
    picked_f = combine_rows(places_f, back_f.reshape(-1, width), top)
    mixed = jnp.sum(weights_f[:, :, None] * picked_f, axis=1)
    layer_out = (xf + mixed).astype(jnp.bfloat16)[None]
    places_b = slot_places(ids_bwd[0], n_exp, cap)
    dnorm = jnp.concatenate(
        [jnp.sum(combine_rows(places_b, part.reshape(n_exp * cap, -1), top), axis=1) for part in back_b], axis=-1
    )
    input_grad = (grad.astype(jnp.float32) + norm_backward(xb, scale_b, gain, dnorm)).astype(
        jnp.bfloat16
    )[None]
    fwd_next = from_behind(layer_out, "pipe", 1)
    bwd_prev = from_behind(input_grad, "pipe", -1)
    return (fwd_next, bwd_prev)


def solution(mesh):
    placed = (
        P("pipe", "ep", None),
        P("pipe", "ep", None),
        P("pipe", "ep", None),
        P("pipe", "ep", None),
        P("pipe", "ep", None),
        P("pipe", "ep", None),
        P("pipe", "ep", None),
        P("pipe", None),
        P("pipe", "ep", None, None),
        P("pipe", "ep", None, None),
        P("pipe", "ep", None, None),
    )
    return jax.shard_map(
        local,
        mesh=mesh,
        in_specs=placed,
        out_specs=(P("pipe", "ep", None), P("pipe", "ep", None)),
        check_vma=False,
    )
```

```python
import jax
import jax.numpy as jnp
from jax import lax
from jax.sharding import PartitionSpec as P

EPS = 1e-06


def from_behind(block, axis, distance):
    devices = range(lax.axis_size(axis))
    route = [((i - distance) % len(devices), i) for i in devices]
    return lax.ppermute(block, axis, route)


def slot_places(ids, n_exp, cap):
    flat = ids.reshape(-1)
    onehot = (flat[:, None] == jnp.arange(n_exp, dtype=jnp.int32)[None, :]).astype(jnp.int32)
    before = jnp.cumsum(onehot, axis=0) - onehot
    slot = jnp.sum(before * onehot, axis=1)
    return flat * cap + slot


def rms_stats(x):
    xf = x.astype(jnp.float32)
    scale = lax.rsqrt(jnp.mean(xf * xf, axis=-1, keepdims=True) + EPS)
    return (xf, scale)


def expert_forward(rows, w_g, w_u, w_d):
    gate = jnp.dot(rows, w_g, preferred_element_type=jnp.float32)
    upper = jnp.dot(rows, w_u, preferred_element_type=jnp.float32)
    act = (jax.nn.silu(gate) * upper).astype(jnp.bfloat16)
    return jnp.dot(act, w_d, preferred_element_type=jnp.float32).astype(jnp.bfloat16)


def expert_backward(rows, cot, w_g, w_u, w_d):
    gate = jnp.dot(rows, w_g, preferred_element_type=jnp.float32)
    upper = jnp.dot(rows, w_u, preferred_element_type=jnp.float32)
    sigma = jax.nn.sigmoid(gate)
    dact = jnp.dot(cot, w_d.T, preferred_element_type=jnp.float32)
    dgate = (dact * upper * sigma * (1.0 + gate * (1.0 - sigma))).astype(jnp.bfloat16)
    dup = (dact * gate * sigma).astype(jnp.bfloat16)
    total = jnp.dot(dgate, w_g.T, preferred_element_type=jnp.float32) + jnp.dot(
        dup, w_u.T, preferred_element_type=jnp.float32
    )
    return total.astype(jnp.bfloat16)


def expert_backward_parts(rows, cot, w_g, w_u, w_d, parts):
    gate = jnp.dot(rows, w_g, preferred_element_type=jnp.float32)
    upper = jnp.dot(rows, w_u, preferred_element_type=jnp.float32)
    sigma = jax.nn.sigmoid(gate)
    dact = jnp.dot(cot, w_d.T, preferred_element_type=jnp.float32)
    dgate = (dact * upper * sigma * (1.0 + gate * (1.0 - sigma))).astype(jnp.bfloat16)
    dup = (dact * gate * sigma).astype(jnp.bfloat16)
    step = w_g.shape[0] // parts
    out = []
    for p in range(parts):
        cols = slice(p * step, (p + 1) * step)
        total = jnp.dot(dgate, w_g[cols].T, preferred_element_type=jnp.float32) + jnp.dot(
            dup, w_u[cols].T, preferred_element_type=jnp.float32
        )
        out.append(total.astype(jnp.bfloat16))
    return out


def norm_backward(xf, scale, gain, upstream):
    scaled = gain * upstream
    inner = jnp.mean(xf * scaled, axis=-1, keepdims=True)
    return scale * scaled - xf * (scale * scale * scale) * inner


def expert_slots(ids_all, weights_all, me, cap):
    match = ids_all == me
    chosen = jnp.any(match, axis=-1)
    weight = jnp.sum(jnp.where(match, weights_all, 0.0), axis=-1)
    pos = jnp.cumsum(chosen.astype(jnp.int32), axis=1) - chosen.astype(jnp.int32)
    slot = jnp.arange(cap, dtype=jnp.int32)[None, :, None]
    onehot = chosen[:, None, :] & (pos[:, None, :] == slot)
    slot_w = jnp.sum(jnp.where(onehot, weight[:, None, :], 0.0), axis=-1)
    return onehot.astype(jnp.bfloat16), slot_w


def pick_rows(onehot, rows):
    picked = jnp.einsum("bct,btd->bcd", onehot, rows, preferred_element_type=jnp.float32)
    return picked.astype(jnp.bfloat16)


def combine_rows(places, back, top):
    count = back.shape[0]
    onehot = (places[:, None] == jnp.arange(count, dtype=jnp.int32)[None, :]).astype(jnp.bfloat16)
    picked = jnp.dot(onehot, back, preferred_element_type=jnp.float32)
    return picked.reshape(-1, top, back.shape[1])


def _pairs(n, n2, stage, move):
    out = []
    for i in range(n):
        e1, e2 = i // n2, i % n2
        if stage == 1:
            e1 = move(e1)
        else:
            e2 = move(e2)
        out.append((i, e1 * n2 + e2))
    return out


def gather_chain(parts, axis_name):
    n = lax.axis_size(axis_name)
    n2 = 4
    if n % n2 or any(v.shape[-1] % 128 for v in parts):
        return [lax.all_gather(v, axis_name, axis=0, tiled=False) for v in parts]
    n1 = n // n2
    me = lax.axis_index(axis_name)
    e1, e2 = me // n2, me % n2

    def along(part):
        s1 = jnp.zeros((n1,) + part.shape, part.dtype)
        s1 = lax.dynamic_update_index_in_dim(s1, part, e1, 0)
        for d in range(1, n1):
            got = lax.ppermute(part, axis_name, _pairs(n, n2, 1, lambda a: (a + d) % n1))
            s1 = lax.dynamic_update_index_in_dim(s1, got, (e1 - d) % n1, 0)
        return s1

    def across(s1):
        flip_x = lambda a: a ^ 1
        flip_y = lambda a: a ^ 2
        px = lax.ppermute(s1, axis_name, _pairs(n, n2, 2, flip_x))
        py = lax.ppermute(s1, axis_name, _pairs(n, n2, 2, flip_y))
        h = (s1.shape[-1] // 256) * 128
        d1 = lax.ppermute(px[..., :h], axis_name, _pairs(n, n2, 2, flip_y))
        d2 = lax.ppermute(py[..., h:], axis_name, _pairs(n, n2, 2, flip_x))
        diag = jnp.concatenate([d1, d2], axis=-1)
        s2 = jnp.zeros((n2,) + s1.shape, s1.dtype)
        s2 = lax.dynamic_update_index_in_dim(s2, s1, e2, 0)
        s2 = lax.dynamic_update_index_in_dim(s2, px, e2 ^ 1, 0)
        s2 = lax.dynamic_update_index_in_dim(s2, py, e2 ^ 2, 0)
        s2 = lax.dynamic_update_index_in_dim(s2, diag, e2 ^ 3, 0)
        return jnp.swapaxes(s2, 0, 1).reshape((n,) + s1.shape[1:])

    done = []
    ready = along(parts[0])
    for part in parts[1:]:
        ready, part = lax.optimization_barrier((ready, part))
        done.append(across(ready))
        ready = along(part)
        done[-1], ready = lax.optimization_barrier((done[-1], ready))
    done.append(across(ready))
    return done

def exchange_ep(blocks, axis_name):
    n = lax.axis_size(axis_name)
    me = lax.axis_index(axis_name)
    out = lax.dynamic_update_index_in_dim(
        jnp.zeros_like(blocks), lax.dynamic_index_in_dim(blocks, me, 0, keepdims=False), me, 0
    )
    for d in range(1, n):
        part = lax.dynamic_index_in_dim(blocks, (me + d) % n, 0, keepdims=False)
        got = lax.ppermute(part, axis_name, [(i, (i + d) % n) for i in range(n)])
        out = lax.dynamic_update_index_in_dim(out, got, (me - d) % n, 0)
    return out


def local(
    x_fwd, ids_fwd, route_fwd, x_bwd, grad_bwd, ids_bwd, route_bwd, norm_gain, w_gate, w_up, w_down
):
    n_exp = lax.axis_size("ep")
    me = lax.axis_index("ep")
    tok_dev = x_fwd.shape[1]
    width = x_fwd.shape[2]
    top = ids_fwd.shape[2]
    cap = 3 * tok_dev * top // (2 * n_exp)
    gain = norm_gain[0].astype(jnp.float32)
    w_g = w_gate[0, 0]
    w_u = w_up[0, 0]
    w_d = w_down[0, 0]
    xf, scale_f = rms_stats(x_fwd[0])
    h_f = (xf * scale_f * gain).astype(jnp.bfloat16)
    xb, scale_b = rms_stats(x_bwd[0])
    h_b = (xb * scale_b * gain).astype(jnp.bfloat16)
    grad = grad_bwd[0]
    weights_f = route_fwd[0] / jnp.sum(route_fwd[0], axis=-1, keepdims=True)
    weights_b = route_bwd[0] / jnp.sum(route_bwd[0], axis=-1, keepdims=True)

    def split3(r):
        hi = lax.reduce_precision(r, exponent_bits=8, mantissa_bits=7)
        rest = r - hi
        mid = lax.reduce_precision(rest, exponent_bits=8, mantissa_bits=7)
        return jnp.concatenate([hi, mid, rest - mid], axis=-1).astype(jnp.bfloat16)

    def join3(p):
        p = p.astype(jnp.float32)
        k = p.shape[-1] // 3
        return (p[..., 0:k] + p[..., k:2 * k]) + p[..., 2 * k:3 * k]

    table = jnp.concatenate(
        [ids_fwd[0].astype(jnp.float32), ids_bwd[0].astype(jnp.float32), route_fwd[0], route_bwd[0]], axis=-1
    )
    meta = split3(table)
    pad = (-meta.shape[-1]) % 128
    meta = jnp.concatenate([meta, jnp.zeros((tok_dev, pad), jnp.bfloat16)], axis=-1)
    message_f, all_h_b, all_g = gather_chain([jnp.concatenate([h_f, meta], axis=-1), h_b, grad], "ep")
    all_h_f = message_f[..., 0:width]
    got = join3(message_f[..., width:width + 3 * table.shape[-1]])
    all_ids_f = got[..., 0:top].astype(jnp.int32)
    all_ids_b = got[..., top:2 * top].astype(jnp.int32)
    all_route_f = got[..., 2 * top:3 * top]
    all_route_b = got[..., 3 * top:4 * top]
    all_w_f = all_route_f / jnp.sum(all_route_f, axis=-1, keepdims=True)
    all_w_b = all_route_b / jnp.sum(all_route_b, axis=-1, keepdims=True)

    onehot_f, _ = expert_slots(all_ids_f, all_w_f, me, cap)
    rows = pick_rows(onehot_f, all_h_f).reshape(-1, width)
    made_f = expert_forward(rows, w_g, w_u, w_d).reshape(n_exp, cap, width)
    back_f = lax.all_to_all(made_f, "ep", split_axis=0, concat_axis=0, tiled=True)

    onehot_b, slot_w_b = expert_slots(all_ids_b, all_w_b, me, cap)
    rows = pick_rows(onehot_b, all_h_b).reshape(-1, width)
    g_rows = pick_rows(onehot_b, all_g)
    cots = (slot_w_b[:, :, None] * g_rows.astype(jnp.float32)).astype(jnp.bfloat16).reshape(-1, width)
    parts = 2 if width % 256 == 0 else 1
    made_parts = [m.reshape(n_exp, cap, -1) for m in expert_backward_parts(rows, cots, w_g, w_u, w_d, parts)]
    back_b = [lax.all_to_all(m, "ep", split_axis=0, concat_axis=0, tiled=True) for m in made_parts[:-1]]
    back_b.append(exchange_ep(made_parts[-1], "ep") if parts > 1 else
                  lax.all_to_all(made_parts[-1], "ep", split_axis=0, concat_axis=0, tiled=True))

    places_f = slot_places(ids_fwd[0], n_exp, cap)
    picked_f = combine_rows(places_f, back_f.reshape(-1, width), top)
    mixed = jnp.sum(weights_f[:, :, None] * picked_f, axis=1)
    layer_out = (xf + mixed).astype(jnp.bfloat16)[None]
    places_b = slot_places(ids_bwd[0], n_exp, cap)
    dnorm = jnp.concatenate(
        [jnp.sum(combine_rows(places_b, part.reshape(n_exp * cap, -1), top), axis=1) for part in back_b], axis=-1
    )
    input_grad = (grad.astype(jnp.float32) + norm_backward(xb, scale_b, gain, dnorm)).astype(
        jnp.bfloat16
    )[None]
    fwd_next = from_behind(layer_out, "pipe", 1)
    bwd_prev = from_behind(input_grad, "pipe", -1)
    return (fwd_next, bwd_prev)


def solution(mesh):
    placed = (
        P("pipe", "ep", None),
        P("pipe", "ep", None),
        P("pipe", "ep", None),
        P("pipe", "ep", None),
        P("pipe", "ep", None),
        P("pipe", "ep", None),
        P("pipe", "ep", None),
        P("pipe", None),
        P("pipe", "ep", None, None),
        P("pipe", "ep", None, None),
        P("pipe", "ep", None, None),
    )
    return jax.shard_map(
        local,
        mesh=mesh,
        in_specs=placed,
        out_specs=(P("pipe", "ep", None), P("pipe", "ep", None)),
        check_vma=False,
    )
```
